32 devices in a mesh: section: 4 (over x, core), expert: 8 (over z, y).
Axes of the slice: x: 2, y: 2, z: 4, core: 2. Of those that a mesh axis runs over, the one named last changes fastest.
Arguments:
- w_in: bfloat16 [2, 4, 8, 2048, 512], P(None, 'section', 'expert'), as said below
- w_out: bfloat16 [2, 4, 8, 256, 2048], P(None, 'section', 'expert'), as said below
- grads: bfloat16 [2, 4, 768, 2048], P(None, 'section', 'expert'), may hold values from -6 to 6
- fresh: bfloat16 [1, 2, 768, 2048], P(None, None, 'expert'), may hold values from -6 to 6
- saved: bfloat16 [2, 2, 4, 8, 192, 2048], P(None, None, 'section', 'expert'), may hold values from -6 to 6
- probs: float32 [2, 2, 4, 768], P(None, None, 'section', 'expert'), may hold values from 0.25 to 1
- routes: int32 [2, 2, 4, 768], P(None, None, 'section', 'expert'), may hold values from 0 to 7, as said below
- counts: int32 [2, 2, 4, 8, 8], P(None, None, 'section', 'expert'), may hold values from 0 to 24, as said below
Outputs:
- out_grads: bfloat16 [2, 4, 768, 2048], P(None, 'section', 'expert')
- grad_in: bfloat16 [4, 8, 2048, 512], P('section', 'expert')
- grad_out: bfloat16 [4, 8, 256, 2048], P('section', 'expert')
The draws below stay inside these ranges and needn't reach their ends.
Inputs may be any that keep to these rules, and one draw needn't show every extreme that they name: `routes`: rows of one source device in a slot are in order of expert: row r goes to expert e when the counts of experts below e sum to r or less and those up to e to more than r. The counts of one source device in a slot sum to 96; in every slot some expert gets 24 rows from every source device. w_in[1, s] equals w_in[0, 3 - s]. w_out[1, s] equals w_out[0, 3 - s].
All inputs are finite; a program needn't handle non-finite values.
Results may differ from the reference program's by a relative error of at most 0.0066.
Values may be sent and summed in bfloat16 or wider, within the bound.
No kernel may reach another device: no remote copies, remote signals or barrier semaphores. Data moves between devices by JAX's collectives and lax.ppermute only.
A program may use at most 128 MiB of HBM per device.

```python
import math
import jax
import jax.numpy as jnp
from jax import lax

D = 2048
H = 256
TOK_DEV = 96
TICKS = 2
EXPERTS = 8
CAP = 24
SLOT = 192
TOKENS = 768
N_SECTION = 4


def draw_w_in(key, part):
    layers = jax.random.normal(key, (N_SECTION, EXPERTS, D, 2 * H), jnp.float32) * D ** (-0.5)
    return jnp.stack([layers, jnp.flip(layers, 0)]).astype(jnp.bfloat16)


def draw_w_out(key, part):
    layers = jax.random.normal(key, (N_SECTION, EXPERTS, H, D), jnp.float32) * H ** (-0.5)
    return jnp.stack([layers, jnp.flip(layers, 0)]).astype(jnp.bfloat16)


def route_tables(key):
    total_slots = TICKS * 2 * N_SECTION
    busy_key, pair_key, order_key = jax.random.split(jax.random.fold_in(key, 11), 3)
    busiest = jax.random.randint(busy_key, (total_slots, 1, 1), 0, EXPERTS).astype(jnp.int32)
    lower_half = jax.random.randint(pair_key, (total_slots, EXPERTS, (EXPERTS - 2) // 2), 0, CAP + 1).astype(jnp.int32)
    full_slot = jnp.full((total_slots, EXPERTS, 1), CAP, jnp.int32)
    empty_slot = jnp.zeros((total_slots, EXPERTS, 1), jnp.int32)
    by_rank = jnp.concatenate([full_slot, empty_slot, lower_half, CAP - lower_half], axis=2)
    order_keys = jax.random.split(order_key, total_slots * EXPERTS)
    ordering = jax.vmap(lambda subkey: jax.random.permutation(subkey, EXPERTS))(order_keys)
    ordering = ordering.reshape(total_slots, EXPERTS, EXPERTS).astype(jnp.int32)
    rank_ids = jnp.arange(EXPERTS, dtype=jnp.int32)
    busy_rank = jnp.argmax(ordering == busiest, axis=2).astype(jnp.int32)
    leading = ordering[:, :, :1]
    ordering = jnp.where(rank_ids == busy_rank[:, :, None], leading, ordering)
    ordering = jnp.where(rank_ids == 0, busiest, ordering)
    matches = (ordering[:, :, :, None] == rank_ids).astype(jnp.int32)
    count_table = jnp.sum(matches * by_rank[:, :, :, None], axis=2).astype(jnp.int32)
    bound_ends = jnp.cumsum(count_table, axis=2).astype(jnp.int32)
    positions = jnp.arange(TOK_DEV, dtype=jnp.int32)
    route_ids = jnp.sum((positions[None, None, :, None] >= bound_ends[:, :, None, :]).astype(jnp.int32), axis=3)
    return (count_table.reshape(TICKS, 2, N_SECTION, EXPERTS, EXPERTS), route_ids.reshape(TICKS, 2, N_SECTION, EXPERTS * TOK_DEV).astype(jnp.int32))


def draw_counts(key, part):
    return route_tables(key)[0]


def draw_routes(key, part):
    return route_tables(key)[1]


def block_levels(rng, dims, cuts, smallest, top_value):
    gain = 1.0
    for axis_at, shards_of in cuts:
        heights = jax.random.uniform(jax.random.fold_in(jax.random.fold_in(rng, 6), axis_at), (shards_of,), jnp.float32, smallest / len(cuts), top_value / len(cuts))
        gain = gain * jnp.repeat(jnp.exp(heights), dims[axis_at] // shards_of).reshape((-1,) + (1,) * (len(dims) - 1 - axis_at))
    return gain


def bell_draw(stream_key, dims, width, bound, cuts=(), kind=jnp.bfloat16):
    drawn = width * jax.random.normal(stream_key, dims, jnp.float32)
    if cuts:
        drawn = drawn * block_levels(stream_key, dims, cuts, -0.22, 0.18)
    return jnp.clip(drawn, -bound, bound).astype(kind)


def setup_inputs(seed: int = 0) -> dict:
    key_list = jax.random.split(jax.random.key(seed), 9)
    w_in = draw_w_in(jax.random.fold_in(key_list[8], 71), 0)
    w_out = draw_w_out(jax.random.fold_in(key_list[8], 71), 0)
    grads = bell_draw(key_list[2], (2, N_SECTION, TOKENS, D), 1.0, 6.0, ((1, 4), (2, 8)))
    fresh = bell_draw(key_list[3], (TICKS - 1, 2, TOKENS, D), 1.0, 6.0, ((2, 8),))
    saved = bell_draw(key_list[4], (TICKS, 2, N_SECTION, EXPERTS, SLOT, D), 1.0, 6.0, ((2, 4), (3, 8)))
    probs = jnp.clip(jnp.exp(math.log(1.0) - 1.3862944 * jax.random.uniform(key_list[5], (TICKS, 2, N_SECTION, TOKENS), jnp.float32) ** block_levels(key_list[5], (TICKS, 2, N_SECTION, TOKENS), ((2, 4), (3, 8)), -0.2, 0.2)), 0.25, 1.0)
    routes = draw_routes(jax.random.fold_in(key_list[8], 71), 0)
    counts = draw_counts(jax.random.fold_in(key_list[8], 71), 0)
    return dict(w_in=w_in, w_out=w_out, grads=grads, fresh=fresh, saved=saved, probs=probs, routes=routes, counts=counts)


def slot_index(route_ids, count_table):
    sources = count_table.shape[0]
    experts = count_table.shape[1]
    rows_each = route_ids.shape[0] // sources
    capacity = 2 * rows_each // experts
    grouped = route_ids.reshape(sources, rows_each).astype(jnp.int32)
    offset = (jnp.cumsum(count_table, axis=1) - count_table).astype(jnp.int32)
    labels = jnp.arange(experts, dtype=jnp.int32)
    matching = grouped[:, :, None] == labels[None, None, :]
    first_slot = jnp.sum(jnp.where(matching, offset[:, None, :], 0), axis=2).astype(jnp.int32)
    within = jnp.arange(rows_each, dtype=jnp.int32)[None, :] - first_slot
    source_ids = jnp.arange(sources, dtype=jnp.int32)[:, None]
    return (grouped * (sources * capacity) + source_ids * capacity + within).reshape(-1).astype(jnp.int32)


def section_backward(operands):
    weight_in, weight_out, gradient, prob_rows, route_ids, count_table, saved_rows = operands
    experts, slot_rows, model_width = saved_rows.shape
    hidden_width = weight_out.shape[1]
    slot_ids = slot_index(route_ids, count_table)
    scaled = (prob_rows[:, None] * gradient.astype(jnp.float32)).astype(jnp.bfloat16)
    buffer = jnp.zeros((experts * slot_rows, model_width), jnp.bfloat16).at[slot_ids].set(scaled)
    slope_rows = buffer.reshape(experts, slot_rows, model_width).astype(jnp.float32)
    inputs = saved_rows.astype(jnp.float32)
    in_matrix = weight_in.astype(jnp.float32)
    out_matrix = weight_out.astype(jnp.float32)
    gate_up = jnp.einsum("esd,edk->esk", inputs, in_matrix)
    gate_part = gate_up[:, :, :hidden_width]
    upward = gate_up[:, :, hidden_width:]
    sigmoid_gate = jax.nn.sigmoid(gate_part)
    active = gate_part * sigmoid_gate
    hidden = (active * upward).astype(jnp.bfloat16)
    hidden_grad = jnp.einsum("esd,ehd->esh", slope_rows, out_matrix)
    gate_grad = hidden_grad * upward * sigmoid_gate * (1.0 + gate_part * (1.0 - sigmoid_gate))
    pair_grad = jnp.concatenate([gate_grad, hidden_grad * active], axis=2).astype(jnp.bfloat16)
    pair_float = pair_grad.astype(jnp.float32)
    input_grad = jnp.einsum("esk,edk->esd", pair_float, in_matrix).astype(jnp.bfloat16)
    part_in = jnp.einsum("esd,esk->edk", inputs, pair_float)
    part_out = jnp.einsum("esh,esd->ehd", hidden.astype(jnp.float32), slope_rows)
    returned = input_grad.reshape(experts * slot_rows, model_width)[slot_ids]
    updated = (gradient.astype(jnp.float32) + returned.astype(jnp.float32)).astype(jnp.bfloat16)
    return updated, part_in, part_out


def reference(w_in, w_out, grads, fresh, saved, probs, routes, counts):
    ticks = saved.shape[0]
    current = [grads[0], grads[1]]
    finished = [grads[0], grads[1]]
    totals_in = [None, None]
    totals_out = [None, None]
    for tick_id in range(ticks):
        for way_id in range(2):
            updated, part_in, part_out = lax.map(section_backward, (w_in[way_id], w_out[way_id], current[way_id], probs[tick_id, way_id], routes[tick_id, way_id], counts[tick_id, way_id], saved[tick_id, way_id]))
            finished[way_id] = updated
            if tick_id == 0:
                totals_in[way_id] = part_in
                totals_out[way_id] = part_out
            else:
                totals_in[way_id] = totals_in[way_id] + part_in
                totals_out[way_id] = totals_out[way_id] + part_out
        if tick_id + 1 < ticks:
            current = [jnp.concatenate([finished[0][1:], fresh[tick_id, 0][None]], axis=0),
                       jnp.concatenate([fresh[tick_id, 1][None], finished[1][:-1]], axis=0)]
    mirror_in = lax.optimization_barrier(jnp.flip(totals_in[1], 0).astype(jnp.bfloat16))
    mirror_out = lax.optimization_barrier(jnp.flip(totals_out[1], 0).astype(jnp.bfloat16))
    grad_in = (totals_in[0] + mirror_in.astype(jnp.float32)).astype(jnp.bfloat16)
    grad_out = (totals_out[0] + mirror_out.astype(jnp.float32)).astype(jnp.bfloat16)
    return jnp.stack(finished), grad_in, grad_out
```

```python
import jax
import jax.numpy as jnp
from jax import lax
from jax.sharding import PartitionSpec as P


def passed_along(block, axis, distance):
    devices = range(lax.axis_size(axis))
    route = [(i - distance, i) for i in devices if i - distance in devices]
    return lax.ppermute(block, axis, route)


def mirrored(block, axis):
    count = lax.axis_size(axis)
    return lax.ppermute(block, axis, [(i, count - 1 - i) for i in range(count)])


def slot_index(route_ids, count_table, capacity):
    experts = count_table.shape[0]
    offset = jnp.cumsum(count_table) - count_table
    labels = lax.iota(jnp.int32, experts)
    first_slot = jnp.sum(
        jnp.where(route_ids[:, None] == labels[None, :], offset[None, :], 0), axis=1
    )
    return route_ids * capacity + lax.iota(jnp.int32, route_ids.shape[0]) - first_slot


def left_product(left, right):
    return lax.dot_general(
        left, right, (((0,), (0,)), ((), ())), preferred_element_type=jnp.float32
    )


def right_product(left, right):
    return lax.dot_general(
        left, right, (((1,), (1,)), ((), ())), preferred_element_type=jnp.float32
    )


def dispatch(gradient, prob_rows, route_ids, count_table):
    tokens, model_width = gradient.shape
    experts = count_table.shape[0]
    capacity = 2 * tokens // experts
    slot_ids = slot_index(route_ids, count_table, capacity)
    scaled = (prob_rows[:, None] * gradient.astype(jnp.float32)).astype(jnp.bfloat16)
    outgoing = jnp.zeros((experts * capacity, model_width), jnp.bfloat16).at[slot_ids].set(scaled)
    arrived = lax.all_to_all(
        outgoing.reshape(experts, capacity, model_width),
        "expert",
        split_axis=0,
        concat_axis=0,
        tiled=True,
    )
    return arrived.reshape(-1, model_width), slot_ids


def expert_grads(slope_rows, saved_rows, weight_in, weight_out):
    hidden_width = weight_out.shape[0]
    gate_up = jnp.dot(saved_rows, weight_in, preferred_element_type=jnp.float32)
    gate_part = gate_up[:, :hidden_width]
    upward = gate_up[:, hidden_width:]
    sigmoid_gate = jax.nn.sigmoid(gate_part)
    active = gate_part * sigmoid_gate
    hidden = (active * upward).astype(jnp.bfloat16)
    hidden_grad = right_product(slope_rows, weight_out)
    gate_grad = hidden_grad * upward * sigmoid_gate * (1.0 + gate_part * (1.0 - sigmoid_gate))
    pair_grad = jnp.concatenate([gate_grad, hidden_grad * active], axis=1).astype(jnp.bfloat16)
    return hidden, pair_grad


def combine(gradient, pair_grad, weight_in, slot_ids):
    experts_rows, model_width = pair_grad.shape[0], gradient.shape[1]
    experts = lax.axis_size("expert")
    input_grad = right_product(pair_grad, weight_in).astype(jnp.bfloat16)
    returned = lax.all_to_all(
        input_grad.reshape(experts, experts_rows // experts, model_width),
        "expert",
        split_axis=0,
        concat_axis=0,
        tiled=True,
    )
    back_rows = jnp.take(returned.reshape(-1, model_width), slot_ids, axis=0)
    return (gradient.astype(jnp.float32) + back_rows.astype(jnp.float32)).astype(jnp.bfloat16)


def weight_terms(saved_rows, slope_rows, hidden, pair_grad):
    return left_product(saved_rows, pair_grad), left_product(hidden, slope_rows)


def on_device(w_in, w_out, grads, fresh, saved, probs, routes, counts):
    sections = lax.axis_size("section")
    section_id = lax.axis_index("section")
    model_width = grads.shape[-1]
    hidden_width = w_out.shape[-2]
    ticks = saved.shape[0]
    saved_mirror = mirrored(saved[:, 1, 0, 0], "section")
    current = [grads[0, 0], grads[1, 0]]
    finished = [grads[0, 0], grads[1, 0]]
    zeros_in = jnp.zeros((model_width, 2 * hidden_width), jnp.float32)
    zeros_out = jnp.zeros((hidden_width, model_width), jnp.float32)
    own_in, own_out = zeros_in, zeros_out
    mirror_in, mirror_out = zeros_in, zeros_out
    for tick_id in range(ticks):
        for way_id in range(2):
            saved_rows = saved[tick_id, way_id, 0, 0]
            slope_rows, slot_ids = dispatch(
                current[way_id],
                probs[tick_id, way_id, 0],
                routes[tick_id, way_id, 0],
                counts[tick_id, way_id, 0, 0],
            )
            hidden, pair_grad = expert_grads(
                slope_rows, saved_rows, w_in[way_id, 0, 0], w_out[way_id, 0, 0]
            )
            finished[way_id] = combine(current[way_id], pair_grad, w_in[way_id, 0, 0], slot_ids)
            if way_id == 0:
                part_in, part_out = weight_terms(saved_rows, slope_rows, hidden, pair_grad)
                own_in = own_in + part_in
                own_out = own_out + part_out
            else:
                slope_mirror = mirrored(slope_rows, "section")
                hidden_m, pair_grad_m = expert_grads(
                    slope_mirror, saved_mirror[tick_id], w_in[0, 0, 0], w_out[0, 0, 0]
                )
                part_in, part_out = weight_terms(
                    saved_mirror[tick_id], slope_mirror, hidden_m, pair_grad_m
                )
                mirror_in = mirror_in + part_in
                mirror_out = mirror_out + part_out
        if tick_id + 1 < ticks:
            from_above = passed_along(finished[0], "section", -1)
            from_below = passed_along(finished[1], "section", 1)
            current = [
                jnp.where(section_id == sections - 1, fresh[tick_id, 0], from_above),
                jnp.where(section_id == 0, fresh[tick_id, 1], from_below),
            ]
    mirror_in = mirror_in.astype(jnp.bfloat16).astype(jnp.float32)
    mirror_out = mirror_out.astype(jnp.bfloat16).astype(jnp.float32)
    grad_in = (own_in + mirror_in).astype(jnp.bfloat16)
    grad_out = (own_out + mirror_out).astype(jnp.bfloat16)
    return (jnp.stack(finished)[:, None], grad_in[None, None], grad_out[None, None])


def solution(mesh):
    return jax.shard_map(
        on_device,
        mesh=mesh,
        in_specs=(
            P(None, "section", "expert", None, None),
            P(None, "section", "expert", None, None),
            P(None, "section", "expert", None),
            P(None, None, "expert", None),
            P(None, None, "section", "expert", None, None),
            P(None, None, "section", "expert"),
            P(None, None, "section", "expert"),
            P(None, None, "section", "expert", None),
        ),
        out_specs=(
            P(None, "section", "expert", None),
            P("section", "expert", None, None),
            P("section", "expert", None, None),
        ),
        check_vma=False,
    )
```

```python
import jax
import jax.numpy as jnp
from jax import lax
from jax.sharding import PartitionSpec as P


def passed_along(block, axis, distance):
    devices = range(lax.axis_size(axis))
    route = [(i - distance, i) for i in devices if i - distance in devices]
    return lax.ppermute(block, axis, route)


def mirrored(block, axis):
    count = lax.axis_size(axis)
    return lax.ppermute(block, axis, [(i, count - 1 - i) for i in range(count)])


def slot_index(route_ids, count_table, capacity):
    experts = count_table.shape[0]
    offset = jnp.cumsum(count_table) - count_table
    labels = lax.iota(jnp.int32, experts)
    first_slot = jnp.sum(
        jnp.where(route_ids[:, None] == labels[None, :], offset[None, :], 0), axis=1
    )
    return route_ids * capacity + lax.iota(jnp.int32, route_ids.shape[0]) - first_slot


def left_product(left, right):
    return lax.dot_general(
        left, right, (((0,), (0,)), ((), ())), preferred_element_type=jnp.float32
    )


def right_product(left, right):
    return lax.dot_general(
        left, right, (((1,), (1,)), ((), ())), preferred_element_type=jnp.float32
    )


def dispatch(gradient, prob_rows, route_ids, count_table):
    tokens, model_width = gradient.shape
    experts = count_table.shape[0]
    capacity = 2 * tokens // experts
    slot_ids = slot_index(route_ids, count_table, capacity)
    scaled = (prob_rows[:, None] * gradient.astype(jnp.float32)).astype(jnp.bfloat16)
    outgoing = jnp.zeros((experts * capacity, model_width), jnp.bfloat16).at[slot_ids].set(scaled)
    arrived = lax.all_to_all(
        outgoing.reshape(experts, capacity, model_width),
        "expert",
        split_axis=0,
        concat_axis=0,
        tiled=True,
    )
    return arrived.reshape(-1, model_width), slot_ids


def expert_grads(slope_rows, saved_rows, weight_in, weight_out):
    hidden_width = weight_out.shape[0]
    gate_up = jnp.dot(saved_rows, weight_in, preferred_element_type=jnp.float32)
    gate_part = gate_up[:, :hidden_width]
    upward = gate_up[:, hidden_width:]
    sigmoid_gate = jax.nn.sigmoid(gate_part)
    active = gate_part * sigmoid_gate
    hidden = (active * upward).astype(jnp.bfloat16)
    hidden_grad = right_product(slope_rows, weight_out)
    gate_grad = hidden_grad * upward * sigmoid_gate * (1.0 + gate_part * (1.0 - sigmoid_gate))
    pair_grad = jnp.concatenate([gate_grad, hidden_grad * active], axis=1).astype(jnp.bfloat16)
    return hidden, pair_grad


def combine(gradient, pair_grad, weight_in, slot_ids, held):
    experts_rows, model_width = pair_grad.shape[0], gradient.shape[1]
    experts = lax.axis_size("expert")
    input_grad = right_product(pair_grad, weight_in).astype(jnp.bfloat16)
    input_grad, held = lax.optimization_barrier((input_grad, held))
    returned = lax.all_to_all(
        input_grad.reshape(experts, experts_rows // experts, model_width),
        "expert",
        split_axis=0,
        concat_axis=0,
        tiled=True,
    )
    back_rows = jnp.take(returned.reshape(-1, model_width), slot_ids, axis=0)
    updated = (gradient.astype(jnp.float32) + back_rows.astype(jnp.float32)).astype(jnp.bfloat16)
    return updated, held


def weight_terms(saved_rows, slope_rows, hidden, pair_grad):
    return left_product(saved_rows, pair_grad), left_product(hidden, slope_rows)


def on_device(w_in, w_out, grads, fresh, saved, probs, routes, counts):
    sections = lax.axis_size("section")
    section_id = lax.axis_index("section")
    model_width = grads.shape[-1]
    hidden_width = w_out.shape[-2]
    ticks = saved.shape[0]
    saved_mirror = mirrored(saved[:, 1, 0, 0], "section")
    current = [grads[0, 0], grads[1, 0]]
    finished = [grads[0, 0], grads[1, 0]]
    zeros_in = jnp.zeros((model_width, 2 * hidden_width), jnp.float32)
    zeros_out = jnp.zeros((hidden_width, model_width), jnp.float32)
    own_in, own_out = zeros_in, zeros_out
    mirror_in, mirror_out = zeros_in, zeros_out
    for tick_id in range(ticks):
        for way_id in range(2):
            saved_rows = saved[tick_id, way_id, 0, 0]
            slope_rows, slot_ids = dispatch(
                current[way_id],
                probs[tick_id, way_id, 0],
                routes[tick_id, way_id, 0],
                counts[tick_id, way_id, 0, 0],
            )
            hidden, pair_grad = expert_grads(
                slope_rows, saved_rows, w_in[way_id, 0, 0], w_out[way_id, 0, 0]
            )
            if way_id == 0:
                finished[0], saved_mirror = combine(
                    current[0], pair_grad, w_in[0, 0, 0], slot_ids, saved_mirror
                )
                part_in, part_out = weight_terms(saved_rows, slope_rows, hidden, pair_grad)
                own_in = own_in + part_in
                own_out = own_out + part_out
            else:
                slope_mirror = mirrored(slope_rows, "section")
                finished[1], slope_mirror = combine(
                    current[1], pair_grad, w_in[1, 0, 0], slot_ids, slope_mirror
                )
                hidden_m, pair_grad_m = expert_grads(
                    slope_mirror, saved_mirror[tick_id], w_in[0, 0, 0], w_out[0, 0, 0]
                )
                part_in, part_out = weight_terms(
                    saved_mirror[tick_id], slope_mirror, hidden_m, pair_grad_m
                )
                mirror_in = mirror_in + part_in
                mirror_out = mirror_out + part_out
        if tick_id + 1 < ticks:
            from_above = passed_along(finished[0], "section", -1)
            from_below = passed_along(finished[1], "section", 1)
            current = [
                jnp.where(section_id == sections - 1, fresh[tick_id, 0], from_above),
                jnp.where(section_id == 0, fresh[tick_id, 1], from_below),
            ]
    mirror_in = mirror_in.astype(jnp.bfloat16).astype(jnp.float32)
    mirror_out = mirror_out.astype(jnp.bfloat16).astype(jnp.float32)
    grad_in = (own_in + mirror_in).astype(jnp.bfloat16)
    grad_out = (own_out + mirror_out).astype(jnp.bfloat16)
    return (jnp.stack(finished)[:, None], grad_in[None, None], grad_out[None, None])


def solution(mesh):
    return jax.shard_map(
        on_device,
        mesh=mesh,
        in_specs=(
            P(None, "section", "expert", None, None),
            P(None, "section", "expert", None, None),
            P(None, "section", "expert", None),
            P(None, None, "expert", None),
            P(None, None, "section", "expert", None, None),
            P(None, None, "section", "expert"),
            P(None, None, "section", "expert"),
            P(None, None, "section", "expert", None),
        ),
        out_specs=(
            P(None, "section", "expert", None),
            P("section", "expert", None, None),
            P("section", "expert", None, None),
        ),
        check_vma=False,
    )
```

```python
import jax
import jax.numpy as jnp
from jax import lax
from jax.sharding import PartitionSpec as P


def passed_along(block, axis, distance):
    devices = range(lax.axis_size(axis))
    route = [(i - distance, i) for i in devices if i - distance in devices]
    return lax.ppermute(block, axis, route)


def mirrored(block, axis):
    count = lax.axis_size(axis)
    return lax.ppermute(block, axis, [(i, count - 1 - i) for i in range(count)])


def slot_index(route_ids, count_table, capacity):
    experts = count_table.shape[0]
    offset = jnp.cumsum(count_table) - count_table
    labels = lax.iota(jnp.int32, experts)
    first_slot = jnp.sum(
        jnp.where(route_ids[:, None] == labels[None, :], offset[None, :], 0), axis=1
    )
    return route_ids * capacity + lax.iota(jnp.int32, route_ids.shape[0]) - first_slot


def left_product(left, right):
    return lax.dot_general(
        left, right, (((0,), (0,)), ((), ())), preferred_element_type=jnp.float32
    )


def right_product(left, right):
    return lax.dot_general(
        left, right, (((1,), (1,)), ((), ())), preferred_element_type=jnp.float32
    )


def outgoing_rows(gradient, prob_rows, route_ids, count_table):
    tokens, model_width = gradient.shape
    experts = count_table.shape[0]
    capacity = 2 * tokens // experts
    slot_ids = slot_index(route_ids, count_table, capacity)
    scaled = (prob_rows[:, None] * gradient.astype(jnp.float32)).astype(jnp.bfloat16)
    outgoing = jnp.zeros((experts * capacity, model_width), jnp.bfloat16).at[slot_ids].set(scaled)
    return outgoing.reshape(experts, 1, capacity, model_width), slot_ids


def exchange(blocks):
    experts, ways, capacity, model_width = blocks.shape
    arrived = lax.all_to_all(blocks, "expert", split_axis=0, concat_axis=0, tiled=True)
    return [arrived[:, way_id].reshape(experts * capacity, model_width) for way_id in range(ways)]


def expert_grads(slope_rows, saved_rows, weight_in, weight_out):
    hidden_width = weight_out.shape[0]
    gate_up = jnp.dot(saved_rows, weight_in, preferred_element_type=jnp.float32)
    gate_part = gate_up[:, :hidden_width]
    upward = gate_up[:, hidden_width:]
    sigmoid_gate = jax.nn.sigmoid(gate_part)
    active = gate_part * sigmoid_gate
    hidden = (active * upward).astype(jnp.bfloat16)
    hidden_grad = right_product(slope_rows, weight_out)
    gate_grad = hidden_grad * upward * sigmoid_gate * (1.0 + gate_part * (1.0 - sigmoid_gate))
    pair_grad = jnp.concatenate([gate_grad, hidden_grad * active], axis=1).astype(jnp.bfloat16)
    return hidden, pair_grad


def weight_terms(saved_rows, slope_rows, hidden, pair_grad):
    return left_product(saved_rows, pair_grad), left_product(hidden, slope_rows)


def on_device(w_in, w_out, grads, fresh, saved, probs, routes, counts):
    sections = lax.axis_size("section")
    section_id = lax.axis_index("section")
    experts = lax.axis_size("expert")
    model_width = grads.shape[-1]
    hidden_width = w_out.shape[-2]
    ticks = saved.shape[0]
    saved_mirror = mirrored(saved[:, 1, 0, 0], "section")
    current = [grads[0, 0], grads[1, 0]]
    zeros_in = jnp.zeros((model_width, 2 * hidden_width), jnp.float32)
    zeros_out = jnp.zeros((hidden_width, model_width), jnp.float32)
    own_in, own_out = zeros_in, zeros_out
    mirror_in, mirror_out = zeros_in, zeros_out
    slope_mirror = None
    for tick_id in range(ticks):
        sent = [
            outgoing_rows(
                current[way_id],
                probs[tick_id, way_id, 0],
                routes[tick_id, way_id, 0],
                counts[tick_id, way_id, 0, 0],
            )
            for way_id in range(2)
        ]
        blocks = jnp.concatenate([sent[0][0], sent[1][0]], axis=1)
        if slope_mirror is not None:
            blocks, slope_mirror = lax.optimization_barrier((blocks, slope_mirror))
            hidden_m, pair_grad_m = expert_grads(
                slope_mirror, saved_mirror[tick_id - 1], w_in[0, 0, 0], w_out[0, 0, 0]
            )
            part_in, part_out = weight_terms(
                saved_mirror[tick_id - 1], slope_mirror, hidden_m, pair_grad_m
            )
            mirror_in = mirror_in + part_in
            mirror_out = mirror_out + part_out
        slopes = exchange(blocks)
        input_grads = []
        for way_id in range(2):
            saved_rows = saved[tick_id, way_id, 0, 0]
            hidden, pair_grad = expert_grads(
                slopes[way_id], saved_rows, w_in[way_id, 0, 0], w_out[way_id, 0, 0]
            )
            input_grad = right_product(pair_grad, w_in[way_id, 0, 0]).astype(jnp.bfloat16)
            input_grads.append(input_grad.reshape(experts, 1, -1, model_width))
            if way_id == 0:
                part_in, part_out = weight_terms(saved_rows, slopes[0], hidden, pair_grad)
                own_in = own_in + part_in
                own_out = own_out + part_out
        slope_mirror = mirrored(slopes[1], "section")
        back_blocks = jnp.concatenate(input_grads, axis=1)
        if tick_id == 0:
            back_blocks, saved_mirror = lax.optimization_barrier((back_blocks, saved_mirror))
        returned = exchange(back_blocks)
        finished = []
        for way_id in range(2):
            back_rows = jnp.take(returned[way_id], sent[way_id][1], axis=0)
            finished.append(
                (current[way_id].astype(jnp.float32) + back_rows.astype(jnp.float32)).astype(
                    jnp.bfloat16
                )
            )
        if tick_id + 1 < ticks:
            from_above = passed_along(finished[0], "section", -1)
            from_below = passed_along(finished[1], "section", 1)
            current = [
                jnp.where(section_id == sections - 1, fresh[tick_id, 0], from_above),
                jnp.where(section_id == 0, fresh[tick_id, 1], from_below),
            ]
    hidden_m, pair_grad_m = expert_grads(
        slope_mirror, saved_mirror[ticks - 1], w_in[0, 0, 0], w_out[0, 0, 0]
    )
    part_in, part_out = weight_terms(saved_mirror[ticks - 1], slope_mirror, hidden_m, pair_grad_m)
    mirror_in = (mirror_in + part_in).astype(jnp.bfloat16).astype(jnp.float32)
    mirror_out = (mirror_out + part_out).astype(jnp.bfloat16).astype(jnp.float32)
    grad_in = (own_in + mirror_in).astype(jnp.bfloat16)
    grad_out = (own_out + mirror_out).astype(jnp.bfloat16)
    return (jnp.stack(finished)[:, None], grad_in[None, None], grad_out[None, None])


def solution(mesh):
    return jax.shard_map(
        on_device,
        mesh=mesh,
        in_specs=(
            P(None, "section", "expert", None, None),
            P(None, "section", "expert", None, None),
            P(None, "section", "expert", None),
            P(None, None, "expert", None),
            P(None, None, "section", "expert", None, None),
            P(None, None, "section", "expert"),
            P(None, None, "section", "expert"),
            P(None, None, "section", "expert", None),
        ),
        out_specs=(
            P(None, "section", "expert", None),
            P("section", "expert", None, None),
            P("section", "expert", None, None),
        ),
        check_vma=False,
    )
```

```python
import jax
import jax.numpy as jnp
from jax import lax
from jax.sharding import PartitionSpec as P


def passed_along(block, axis, distance):
    devices = range(lax.axis_size(axis))
    route = [(i - distance, i) for i in devices if i - distance in devices]
    return lax.ppermute(block, axis, route)


def mirrored(block, axis):
    count = lax.axis_size(axis)
    return lax.ppermute(block, axis, [(i, count - 1 - i) for i in range(count)])


def left_product(left, right):
    return lax.dot_general(
        left, right, (((0,), (0,)), ((), ())), preferred_element_type=jnp.float32
    )


def right_product(left, right):
    return lax.dot_general(
        left, right, (((1,), (1,)), ((), ())), preferred_element_type=jnp.float32
    )


def slot_table(route_ids, count_table, capacity, way_id, ways):
    experts = count_table.shape[0]
    labels = lax.iota(jnp.int32, experts)
    below = jnp.sum(
        jnp.where(labels[None, :] < labels[:, None], count_table[None, :], 0), axis=1
    )
    first_slot = jnp.sum(jnp.where(route_ids[:, None] == labels[None, :], below[None, :], 0), axis=1)
    within = lax.iota(jnp.int32, route_ids.shape[0]) - first_slot
    return (route_ids * ways + way_id) * capacity + within


def placement(route_ids, count_tables, capacity):
    ways, tokens = route_ids.shape
    experts = count_tables.shape[1]
    slots = jnp.concatenate(
        [slot_table(route_ids[w], count_tables[w], capacity, w, ways) for w in range(ways)]
    )
    rows = lax.iota(jnp.int32, ways * experts * capacity)
    return (rows[:, None] == slots[None, :]).astype(jnp.bfloat16)


def exchange(blocks):
    experts, ways, capacity, model_width = blocks.shape
    arrived = lax.all_to_all(blocks, "expert", split_axis=0, concat_axis=0, tiled=True)
    return [arrived[:, way_id].reshape(experts * capacity, model_width) for way_id in range(ways)]


def expert_grads(slope_rows, saved_rows, weight_in, weight_out):
    hidden_width = weight_out.shape[0]
    gate_up = jnp.dot(saved_rows, weight_in, preferred_element_type=jnp.float32)
    gate_part = gate_up[:, :hidden_width]
    upward = gate_up[:, hidden_width:]
    sigmoid_gate = jax.nn.sigmoid(gate_part)
    active = gate_part * sigmoid_gate
    hidden = (active * upward).astype(jnp.bfloat16)
    hidden_grad = right_product(slope_rows, weight_out)
    gate_grad = hidden_grad * upward * sigmoid_gate * (1.0 + gate_part * (1.0 - sigmoid_gate))
    pair_grad = jnp.concatenate([gate_grad, hidden_grad * active], axis=1).astype(jnp.bfloat16)
    return hidden, pair_grad


def weight_terms(saved_rows, slope_rows, hidden, pair_grad):
    return left_product(saved_rows, pair_grad), left_product(hidden, slope_rows)


def on_device(w_in, w_out, grads, fresh, saved, probs, routes, counts):
    sections = lax.axis_size("section")
    section_id = lax.axis_index("section")
    experts = lax.axis_size("expert")
    model_width = grads.shape[-1]
    tokens = grads.shape[2]
    capacity = 2 * tokens // experts
    hidden_width = w_out.shape[-2]
    ticks = saved.shape[0]
    saved_mirror = mirrored(saved[:, 1, 0, 0], "section")
    current = grads[:, 0]
    zeros_in = jnp.zeros((model_width, 2 * hidden_width), jnp.float32)
    zeros_out = jnp.zeros((hidden_width, model_width), jnp.float32)
    own_in, own_out = zeros_in, zeros_out
    mirror_in, mirror_out = zeros_in, zeros_out
    slope_mirror = None
    for tick_id in range(ticks):
        one_hot = placement(routes[tick_id, :, 0], counts[tick_id, :, 0, 0], capacity)
        scaled = (probs[tick_id, :, 0][:, :, None] * current.astype(jnp.float32)).astype(jnp.bfloat16)
        blocks = jnp.dot(one_hot, scaled.reshape(-1, model_width), preferred_element_type=jnp.float32)
        blocks = blocks.astype(jnp.bfloat16).reshape(experts, 2, capacity, model_width)
        if slope_mirror is not None:
            blocks, slope_mirror = lax.optimization_barrier((blocks, slope_mirror))
            hidden_m, pair_grad_m = expert_grads(
                slope_mirror, saved_mirror[tick_id - 1], w_in[0, 0, 0], w_out[0, 0, 0]
            )
            part_in, part_out = weight_terms(
                saved_mirror[tick_id - 1], slope_mirror, hidden_m, pair_grad_m
            )
            mirror_in = mirror_in + part_in
            mirror_out = mirror_out + part_out
        slopes = exchange(blocks)
        input_grads = []
        for way_id in range(2):
            saved_rows = saved[tick_id, way_id, 0, 0]
            hidden, pair_grad = expert_grads(
                slopes[way_id], saved_rows, w_in[way_id, 0, 0], w_out[way_id, 0, 0]
            )
            input_grad = right_product(pair_grad, w_in[way_id, 0, 0]).astype(jnp.bfloat16)
            input_grads.append(input_grad.reshape(experts, 1, capacity, model_width))
            if way_id == 0:
                part_in, part_out = weight_terms(saved_rows, slopes[0], hidden, pair_grad)
                own_in = own_in + part_in
                own_out = own_out + part_out
        slope_mirror = mirrored(slopes[1], "section")
        back_blocks = jnp.concatenate(input_grads, axis=1)
        if tick_id == 0:
            back_blocks, saved_mirror = lax.optimization_barrier((back_blocks, saved_mirror))
        returned = lax.all_to_all(back_blocks, "expert", split_axis=0, concat_axis=0, tiled=True)
        back_rows = left_product(one_hot, returned.reshape(-1, model_width))
        finished = (current.astype(jnp.float32) + back_rows.reshape(2, tokens, model_width)).astype(
            jnp.bfloat16
        )
        if tick_id + 1 < ticks:
            from_above = passed_along(finished[0], "section", -1)
            from_below = passed_along(finished[1], "section", 1)
            current = jnp.stack([
                jnp.where(section_id == sections - 1, fresh[tick_id, 0], from_above),
                jnp.where(section_id == 0, fresh[tick_id, 1], from_below),
            ])
    hidden_m, pair_grad_m = expert_grads(
        slope_mirror, saved_mirror[ticks - 1], w_in[0, 0, 0], w_out[0, 0, 0]
    )
    part_in, part_out = weight_terms(saved_mirror[ticks - 1], slope_mirror, hidden_m, pair_grad_m)
    mirror_in = (mirror_in + part_in).astype(jnp.bfloat16).astype(jnp.float32)
    mirror_out = (mirror_out + part_out).astype(jnp.bfloat16).astype(jnp.float32)
    grad_in = (own_in + mirror_in).astype(jnp.bfloat16)
    grad_out = (own_out + mirror_out).astype(jnp.bfloat16)
    return (finished[:, None], grad_in[None, None], grad_out[None, None])


def solution(mesh):
    return jax.shard_map(
        on_device,
        mesh=mesh,
        in_specs=(
            P(None, "section", "expert", None, None),
            P(None, "section", "expert", None, None),
            P(None, "section", "expert", None),
            P(None, None, "expert", None),
            P(None, None, "section", "expert", None, None),
            P(None, None, "section", "expert"),
            P(None, None, "section", "expert"),
            P(None, None, "section", "expert", None),
        ),
        out_specs=(
            P(None, "section", "expert", None),
            P("section", "expert", None, None),
            P("section", "expert", None, None),
        ),
        check_vma=False,
    )
```

```python
import jax
import jax.numpy as jnp
from jax import lax
from jax.sharding import PartitionSpec as P


def passed_along(block, axis, distance):
    devices = range(lax.axis_size(axis))
    route = [(i - distance, i) for i in devices if i - distance in devices]
    return lax.ppermute(block, axis, route)


def mirrored(block, axis):
    count = lax.axis_size(axis)
    return lax.ppermute(block, axis, [(i, count - 1 - i) for i in range(count)])


def left_product(left, right):
    return lax.dot_general(
        left, right, (((0,), (0,)), ((), ())), preferred_element_type=jnp.float32
    )


def right_product(left, right):
    return lax.dot_general(
        left, right, (((1,), (1,)), ((), ())), preferred_element_type=jnp.float32
    )


def slot_table(route_ids, count_table, capacity, way_id, ways):
    experts = count_table.shape[0]
    labels = lax.iota(jnp.int32, experts)
    below = jnp.sum(
        jnp.where(labels[None, :] < labels[:, None], count_table[None, :], 0), axis=1
    )
    first_slot = jnp.sum(jnp.where(route_ids[:, None] == labels[None, :], below[None, :], 0), axis=1)
    within = lax.iota(jnp.int32, route_ids.shape[0]) - first_slot
    return (route_ids * ways + way_id) * capacity + within


def placement(route_ids, count_tables, capacity):
    ways, tokens = route_ids.shape
    experts = count_tables.shape[1]
    slots = jnp.concatenate(
        [slot_table(route_ids[w], count_tables[w], capacity, w, ways) for w in range(ways)]
    )
    rows = lax.iota(jnp.int32, ways * experts * capacity)
    return (rows[:, None] == slots[None, :]).astype(jnp.bfloat16)


def exchange(blocks):
    experts, ways, capacity, model_width = blocks.shape
    arrived = lax.all_to_all(blocks, "expert", split_axis=0, concat_axis=0, tiled=True)
    return [arrived[:, way_id].reshape(experts * capacity, model_width) for way_id in range(ways)]


def expert_grads(slope_rows, saved_rows, weight_in, weight_out):
    hidden_width = weight_out.shape[0]
    gate_up = jnp.dot(saved_rows, weight_in, preferred_element_type=jnp.float32)
    gate_part = gate_up[:, :hidden_width]
    upward = gate_up[:, hidden_width:]
    sigmoid_gate = jax.nn.sigmoid(gate_part)
    active = gate_part * sigmoid_gate
    hidden = (active * upward).astype(jnp.bfloat16)
    hidden_grad = right_product(slope_rows, weight_out)
    gate_grad = hidden_grad * upward * sigmoid_gate * (1.0 + gate_part * (1.0 - sigmoid_gate))
    pair_grad = jnp.concatenate([gate_grad, hidden_grad * active], axis=1).astype(jnp.bfloat16)
    return hidden, pair_grad


def weight_terms(saved_rows, slope_rows, hidden, pair_grad):
    return left_product(saved_rows, pair_grad), left_product(hidden, slope_rows)


def on_device(w_in, w_out, grads, fresh, saved, probs, routes, counts):
    sections = lax.axis_size("section")
    section_id = lax.axis_index("section")
    experts = lax.axis_size("expert")
    model_width = grads.shape[-1]
    tokens = grads.shape[2]
    capacity = 2 * tokens // experts
    hidden_width = w_out.shape[-2]
    ticks = saved.shape[0]
    saved_mirror = mirrored(saved[:, 1, 0, 0], "section")
    current = grads[:, 0]
    zeros_in = jnp.zeros((model_width, 2 * hidden_width), jnp.float32)
    zeros_out = jnp.zeros((hidden_width, model_width), jnp.float32)
    own_in, own_out = zeros_in, zeros_out
    mirror_in, mirror_out = zeros_in, zeros_out
    slope_mirror = None
    for tick_id in range(ticks):
        one_hot = placement(routes[tick_id, :, 0], counts[tick_id, :, 0, 0], capacity)
        scaled = (probs[tick_id, :, 0][:, :, None] * current.astype(jnp.float32)).astype(jnp.bfloat16)
        blocks = jnp.dot(one_hot, scaled.reshape(-1, model_width), preferred_element_type=jnp.float32)
        blocks = blocks.astype(jnp.bfloat16).reshape(experts, 2, capacity, model_width)
        if slope_mirror is not None:
            hidden_m, pair_grad_m = expert_grads(
                slope_mirror, saved_mirror[tick_id - 1], w_in[0, 0, 0], w_out[0, 0, 0]
            )
            part_in, part_out = weight_terms(
                saved_mirror[tick_id - 1], slope_mirror, hidden_m, pair_grad_m
            )
            mirror_in = mirror_in + part_in
            mirror_out = mirror_out + part_out
        slopes = exchange(blocks)
        input_grads = []
        for way_id in range(2):
            saved_rows = saved[tick_id, way_id, 0, 0]
            hidden, pair_grad = expert_grads(
                slopes[way_id], saved_rows, w_in[way_id, 0, 0], w_out[way_id, 0, 0]
            )
            input_grad = right_product(pair_grad, w_in[way_id, 0, 0]).astype(jnp.bfloat16)
            input_grads.append(input_grad.reshape(experts, 1, capacity, model_width))
            if way_id == 0:
                part_in, part_out = weight_terms(saved_rows, slopes[0], hidden, pair_grad)
                own_in = own_in + part_in
                own_out = own_out + part_out
        slope_mirror = mirrored(slopes[1], "section")
        back_blocks = jnp.concatenate(input_grads, axis=1)
        if tick_id == 0:
            back_blocks, saved_mirror = lax.optimization_barrier((back_blocks, saved_mirror))
        returned = lax.all_to_all(back_blocks, "expert", split_axis=0, concat_axis=0, tiled=True)
        if tick_id + 1 < ticks:
            returned, slope_mirror = lax.optimization_barrier((returned, slope_mirror))
        back_rows = left_product(one_hot, returned.reshape(-1, model_width))
        finished = (current.astype(jnp.float32) + back_rows.reshape(2, tokens, model_width)).astype(
            jnp.bfloat16
        )
        if tick_id + 1 < ticks:
            from_above = passed_along(finished[0], "section", -1)
            from_below = passed_along(finished[1], "section", 1)
            current = jnp.stack([
                jnp.where(section_id == sections - 1, fresh[tick_id, 0], from_above),
                jnp.where(section_id == 0, fresh[tick_id, 1], from_below),
            ])
    hidden_m, pair_grad_m = expert_grads(
        slope_mirror, saved_mirror[ticks - 1], w_in[0, 0, 0], w_out[0, 0, 0]
    )
    part_in, part_out = weight_terms(saved_mirror[ticks - 1], slope_mirror, hidden_m, pair_grad_m)
    mirror_in = (mirror_in + part_in).astype(jnp.bfloat16).astype(jnp.float32)
    mirror_out = (mirror_out + part_out).astype(jnp.bfloat16).astype(jnp.float32)
    grad_in = (own_in + mirror_in).astype(jnp.bfloat16)
    grad_out = (own_out + mirror_out).astype(jnp.bfloat16)
    return (finished[:, None], grad_in[None, None], grad_out[None, None])


def solution(mesh):
    return jax.shard_map(
        on_device,
        mesh=mesh,
        in_specs=(
            P(None, "section", "expert", None, None),
            P(None, "section", "expert", None, None),
            P(None, "section", "expert", None),
            P(None, None, "expert", None),
            P(None, None, "section", "expert", None, None),
            P(None, None, "section", "expert"),
            P(None, None, "section", "expert"),
            P(None, None, "section", "expert", None),
        ),
        out_specs=(
            P(None, "section", "expert", None),
            P("section", "expert", None, None),
            P("section", "expert", None, None),
        ),
        check_vma=False,
    )
```

```python
import jax
import jax.numpy as jnp
from jax import lax
from jax.sharding import PartitionSpec as P


def passed_along(block, axis, distance):
    devices = range(lax.axis_size(axis))
    route = [(i - distance, i) for i in devices if i - distance in devices]
    return lax.ppermute(block, axis, route)


def mirrored(block, axis):
    count = lax.axis_size(axis)
    return lax.ppermute(block, axis, [(i, count - 1 - i) for i in range(count)])


def left_product(left, right):
    return lax.dot_general(
        left, right, (((0,), (0,)), ((), ())), preferred_element_type=jnp.float32
    )


def right_product(left, right):
    return lax.dot_general(
        left, right, (((1,), (1,)), ((), ())), preferred_element_type=jnp.float32
    )


def slot_table(route_ids, count_table, capacity, way_id, ways):
    experts = count_table.shape[0]
    labels = lax.iota(jnp.int32, experts)
    below = jnp.sum(
        jnp.where(labels[None, :] < labels[:, None], count_table[None, :], 0), axis=1
    )
    first_slot = jnp.sum(jnp.where(route_ids[:, None] == labels[None, :], below[None, :], 0), axis=1)
    within = lax.iota(jnp.int32, route_ids.shape[0]) - first_slot
    return (route_ids * ways + way_id) * capacity + within


def placement(route_ids, count_tables, capacity):
    ways, tokens = route_ids.shape
    experts = count_tables.shape[1]
    slots = jnp.concatenate(
        [slot_table(route_ids[w], count_tables[w], capacity, w, ways) for w in range(ways)]
    )
    rows = lax.iota(jnp.int32, ways * experts * capacity)
    return (rows[:, None] == slots[None, :]).astype(jnp.bfloat16)


def exchange(blocks, ways):
    experts, rows, model_width = blocks.shape
    capacity = rows // ways
    arrived = lax.all_to_all(blocks, "expert", split_axis=0, concat_axis=0, tiled=True)
    return [
        arrived[:, way_id * capacity:(way_id + 1) * capacity].reshape(experts * capacity, model_width)
        for way_id in range(ways)
    ]


def expert_grads(slope_rows, saved_rows, weight_in, weight_out):
    hidden_width = weight_out.shape[0]
    gate_up = jnp.dot(saved_rows, weight_in, preferred_element_type=jnp.float32)
    gate_part = gate_up[:, :hidden_width]
    upward = gate_up[:, hidden_width:]
    sigmoid_gate = jax.nn.sigmoid(gate_part)
    active = gate_part * sigmoid_gate
    hidden = (active * upward).astype(jnp.bfloat16)
    hidden_grad = right_product(slope_rows, weight_out)
    gate_grad = hidden_grad * upward * sigmoid_gate * (1.0 + gate_part * (1.0 - sigmoid_gate))
    pair_grad = jnp.concatenate([gate_grad, hidden_grad * active], axis=1).astype(jnp.bfloat16)
    return hidden, pair_grad


def weight_terms(saved_rows, slope_rows, hidden, pair_grad):
    return left_product(saved_rows, pair_grad), left_product(hidden, slope_rows)


def on_device(w_in, w_out, grads, fresh, saved, probs, routes, counts):
    sections = lax.axis_size("section")
    section_id = lax.axis_index("section")
    experts = lax.axis_size("expert")
    model_width = grads.shape[-1]
    tokens = grads.shape[2]
    capacity = 2 * tokens // experts
    hidden_width = w_out.shape[-2]
    ticks = saved.shape[0]
    saved_mirror = mirrored(saved[:, 1, 0, 0], "section")
    current = grads[:, 0]
    zeros_in = jnp.zeros((model_width, 2 * hidden_width), jnp.float32)
    zeros_out = jnp.zeros((hidden_width, model_width), jnp.float32)
    own_in, own_out = zeros_in, zeros_out
    mirror_in, mirror_out = zeros_in, zeros_out
    slope_mirror = None
    for tick_id in range(ticks):
        one_hot = placement(routes[tick_id, :, 0], counts[tick_id, :, 0, 0], capacity)
        scaled = (probs[tick_id, :, 0][:, :, None] * current.astype(jnp.float32)).astype(jnp.bfloat16)
        blocks = jnp.dot(one_hot, scaled.reshape(-1, model_width), preferred_element_type=jnp.float32)
        blocks = blocks.astype(jnp.bfloat16).reshape(experts, 2 * capacity, model_width)
        if slope_mirror is not None:
            hidden_m, pair_grad_m = expert_grads(
                slope_mirror, saved_mirror[tick_id - 1], w_in[0, 0, 0], w_out[0, 0, 0]
            )
            part_in, part_out = weight_terms(
                saved_mirror[tick_id - 1], slope_mirror, hidden_m, pair_grad_m
            )
            mirror_in = mirror_in + part_in
            mirror_out = mirror_out + part_out
        slopes = exchange(blocks, 2)
        input_grads = []
        for way_id in range(2):
            saved_rows = saved[tick_id, way_id, 0, 0]
            hidden, pair_grad = expert_grads(
                slopes[way_id], saved_rows, w_in[way_id, 0, 0], w_out[way_id, 0, 0]
            )
            input_grad = right_product(pair_grad, w_in[way_id, 0, 0]).astype(jnp.bfloat16)
            input_grads.append(input_grad.reshape(experts, capacity, model_width))
            if way_id == 0:
                part_in, part_out = weight_terms(saved_rows, slopes[0], hidden, pair_grad)
                own_in = own_in + part_in
                own_out = own_out + part_out
        slope_mirror = mirrored(slopes[1], "section")
        back_blocks = jnp.concatenate(input_grads, axis=1)
        if tick_id == 0:
            back_blocks, saved_mirror = lax.optimization_barrier((back_blocks, saved_mirror))
        returned = lax.all_to_all(back_blocks, "expert", split_axis=0, concat_axis=0, tiled=True)
        if tick_id + 1 < ticks:
            returned, slope_mirror = lax.optimization_barrier((returned, slope_mirror))
        back_rows = left_product(one_hot, returned.reshape(-1, model_width))
        finished = (current.astype(jnp.float32) + back_rows.reshape(2, tokens, model_width)).astype(
            jnp.bfloat16
        )
        if tick_id + 1 < ticks:
            from_above = passed_along(finished[0], "section", -1)
            from_below = passed_along(finished[1], "section", 1)
            current = jnp.stack([
                jnp.where(section_id == sections - 1, fresh[tick_id, 0], from_above),
                jnp.where(section_id == 0, fresh[tick_id, 1], from_below),
            ])
    hidden_m, pair_grad_m = expert_grads(
        slope_mirror, saved_mirror[ticks - 1], w_in[0, 0, 0], w_out[0, 0, 0]
    )
    part_in, part_out = weight_terms(saved_mirror[ticks - 1], slope_mirror, hidden_m, pair_grad_m)
    mirror_in = (mirror_in + part_in).astype(jnp.bfloat16).astype(jnp.float32)
    mirror_out = (mirror_out + part_out).astype(jnp.bfloat16).astype(jnp.float32)
    grad_in = (own_in + mirror_in).astype(jnp.bfloat16)
    grad_out = (own_out + mirror_out).astype(jnp.bfloat16)
    return (finished[:, None], grad_in[None, None], grad_out[None, None])


def solution(mesh):
    return jax.shard_map(
        on_device,
        mesh=mesh,
        in_specs=(
            P(None, "section", "expert", None, None),
            P(None, "section", "expert", None, None),
            P(None, "section", "expert", None),
            P(None, None, "expert", None),
            P(None, None, "section", "expert", None, None),
            P(None, None, "section", "expert"),
            P(None, None, "section", "expert"),
            P(None, None, "section", "expert", None),
        ),
        out_specs=(
            P(None, "section", "expert", None),
            P("section", "expert", None, None),
            P("section", "expert", None, None),
        ),
        check_vma=False,
    )
```

```python
import jax
import jax.numpy as jnp
from jax import lax
from jax.sharding import PartitionSpec as P


def passed_along(block, axis, distance):
    devices = range(lax.axis_size(axis))
    route = [(i - distance, i) for i in devices if i - distance in devices]
    return lax.ppermute(block, axis, route)


def mirrored(block, axis):
    count = lax.axis_size(axis)
    return lax.ppermute(block, axis, [(i, count - 1 - i) for i in range(count)])


def left_product(left, right):
    return lax.dot_general(
        left, right, (((0,), (0,)), ((), ())), preferred_element_type=jnp.float32
    )


def right_product(left, right):
    return lax.dot_general(
        left, right, (((1,), (1,)), ((), ())), preferred_element_type=jnp.float32
    )


def slot_table(route_ids, count_table, capacity, way_id, ways):
    experts = count_table.shape[0]
    labels = lax.iota(jnp.int32, experts)
    below = jnp.sum(
        jnp.where(labels[None, :] < labels[:, None], count_table[None, :], 0), axis=1
    )
    first_slot = jnp.sum(jnp.where(route_ids[:, None] == labels[None, :], below[None, :], 0), axis=1)
    within = lax.iota(jnp.int32, route_ids.shape[0]) - first_slot
    return (route_ids * ways + way_id) * capacity + within


def placement(route_ids, count_tables, capacity):
    ways, tokens = route_ids.shape
    experts = count_tables.shape[1]
    slots = jnp.concatenate(
        [slot_table(route_ids[w], count_tables[w], capacity, w, ways) for w in range(ways)]
    )
    rows = lax.iota(jnp.int32, ways * experts * capacity)
    return (rows[:, None] == slots[None, :]).astype(jnp.bfloat16)


def exchange(blocks, ways):
    experts, rows, model_width = blocks.shape
    capacity = rows // ways
    arrived = lax.all_to_all(blocks, "expert", split_axis=0, concat_axis=0, tiled=True)
    return [
        arrived[:, way_id * capacity:(way_id + 1) * capacity].reshape(experts * capacity, model_width)
        for way_id in range(ways)
    ]


def expert_grads(slope_rows, saved_rows, weight_in, weight_out):
    hidden_width = weight_out.shape[0]
    gate_up = jnp.dot(saved_rows, weight_in, preferred_element_type=jnp.float32)
    gate_part = gate_up[:, :hidden_width]
    upward = gate_up[:, hidden_width:]
    sigmoid_gate = jax.nn.sigmoid(gate_part)
    active = gate_part * sigmoid_gate
    hidden = (active * upward).astype(jnp.bfloat16)
    hidden_grad = right_product(slope_rows, weight_out)
    gate_grad = hidden_grad * upward * sigmoid_gate * (1.0 + gate_part * (1.0 - sigmoid_gate))
    pair_grad = jnp.concatenate([gate_grad, hidden_grad * active], axis=1).astype(jnp.bfloat16)
    return hidden, pair_grad


def weight_terms(saved_rows, slope_rows, hidden, pair_grad):
    return left_product(saved_rows, pair_grad), left_product(hidden, slope_rows)


def on_device(w_in, w_out, grads, fresh, saved, probs, routes, counts):
    sections = lax.axis_size("section")
    section_id = lax.axis_index("section")
    experts = lax.axis_size("expert")
    model_width = grads.shape[-1]
    tokens = grads.shape[2]
    capacity = 2 * tokens // experts
    hidden_width = w_out.shape[-2]
    ticks = saved.shape[0]
    saved_mirror = mirrored(saved[:, 1, 0, 0], "section")
    current = grads[:, 0]
    zeros_in = jnp.zeros((model_width, 2 * hidden_width), jnp.float32)
    zeros_out = jnp.zeros((hidden_width, model_width), jnp.float32)
    own_in, own_out = zeros_in, zeros_out
    mirror_in, mirror_out = zeros_in, zeros_out
    slope_mirror = None
    for tick_id in range(ticks):
        one_hot = placement(routes[tick_id, :, 0], counts[tick_id, :, 0, 0], capacity)
        scaled = (probs[tick_id, :, 0][:, :, None] * current.astype(jnp.float32)).astype(jnp.bfloat16)
        blocks = jnp.dot(one_hot, scaled.reshape(-1, model_width), preferred_element_type=jnp.float32)
        blocks = blocks.astype(jnp.bfloat16).reshape(experts, 2 * capacity, model_width)
        if slope_mirror is not None:
            hidden_m, pair_grad_m = expert_grads(
                slope_mirror, saved_mirror[tick_id - 1], w_in[0, 0, 0], w_out[0, 0, 0]
            )
            part_in, part_out = weight_terms(
                saved_mirror[tick_id - 1], slope_mirror, hidden_m, pair_grad_m
            )
            mirror_in = mirror_in + part_in
            mirror_out = mirror_out + part_out
        slopes = exchange(blocks, 2)
        if tick_id == 0:
            slopes, saved_mirror = lax.optimization_barrier((slopes, saved_mirror))
        input_grads = []
        for way_id in range(2):
            saved_rows = saved[tick_id, way_id, 0, 0]
            hidden, pair_grad = expert_grads(
                slopes[way_id], saved_rows, w_in[way_id, 0, 0], w_out[way_id, 0, 0]
            )
            input_grad = right_product(pair_grad, w_in[way_id, 0, 0]).astype(jnp.bfloat16)
            input_grads.append(input_grad.reshape(experts, capacity, model_width))
            if way_id == 0:
                part_in, part_out = weight_terms(saved_rows, slopes[0], hidden, pair_grad)
                own_in = own_in + part_in
                own_out = own_out + part_out
        slope_mirror = mirrored(slopes[1], "section")
        back_blocks = jnp.concatenate(input_grads, axis=1)
        returned = lax.all_to_all(back_blocks, "expert", split_axis=0, concat_axis=0, tiled=True)
        if tick_id + 1 < ticks:
            returned, slope_mirror = lax.optimization_barrier((returned, slope_mirror))
        back_rows = left_product(one_hot, returned.reshape(-1, model_width))
        finished = (current.astype(jnp.float32) + back_rows.reshape(2, tokens, model_width)).astype(
            jnp.bfloat16
        )
        if tick_id + 1 < ticks:
            from_above = passed_along(finished[0], "section", -1)
            from_below = passed_along(finished[1], "section", 1)
            current = jnp.stack([
                jnp.where(section_id == sections - 1, fresh[tick_id, 0], from_above),
                jnp.where(section_id == 0, fresh[tick_id, 1], from_below),
            ])
    hidden_m, pair_grad_m = expert_grads(
        slope_mirror, saved_mirror[ticks - 1], w_in[0, 0, 0], w_out[0, 0, 0]
    )
    part_in, part_out = weight_terms(saved_mirror[ticks - 1], slope_mirror, hidden_m, pair_grad_m)
    mirror_in = (mirror_in + part_in).astype(jnp.bfloat16).astype(jnp.float32)
    mirror_out = (mirror_out + part_out).astype(jnp.bfloat16).astype(jnp.float32)
    grad_in = (own_in + mirror_in).astype(jnp.bfloat16)
    grad_out = (own_out + mirror_out).astype(jnp.bfloat16)
    return (finished[:, None], grad_in[None, None], grad_out[None, None])


def solution(mesh):
    return jax.shard_map(
        on_device,
        mesh=mesh,
        in_specs=(
            P(None, "section", "expert", None, None),
            P(None, "section", "expert", None, None),
            P(None, "section", "expert", None),
            P(None, None, "expert", None),
            P(None, None, "section", "expert", None, None),
            P(None, None, "section", "expert"),
            P(None, None, "section", "expert"),
            P(None, None, "section", "expert", None),
        ),
        out_specs=(
            P(None, "section", "expert", None),
            P("section", "expert", None, None),
            P("section", "expert", None, None),
        ),
        check_vma=False,
    )
```

```python
import jax
import jax.numpy as jnp
from jax import lax
from jax.sharding import PartitionSpec as P


def passed_along(block, axis, distance):
    devices = range(lax.axis_size(axis))
    route = [(i - distance, i) for i in devices if i - distance in devices]
    return lax.ppermute(block, axis, route)


def mirrored(block, axis):
    count = lax.axis_size(axis)
    return lax.ppermute(block, axis, [(i, count - 1 - i) for i in range(count)])


def left_product(left, right):
    return lax.dot_general(
        left, right, (((0,), (0,)), ((), ())), preferred_element_type=jnp.float32
    )


def right_product(left, right):
    return lax.dot_general(
        left, right, (((1,), (1,)), ((), ())), preferred_element_type=jnp.float32
    )


def slot_table(route_ids, count_table, capacity, way_id, ways):
    experts = count_table.shape[0]
    labels = lax.iota(jnp.int32, experts)
    below = jnp.sum(
        jnp.where(labels[None, :] < labels[:, None], count_table[None, :], 0), axis=1
    )
    first_slot = jnp.sum(jnp.where(route_ids[:, None] == labels[None, :], below[None, :], 0), axis=1)
    within = lax.iota(jnp.int32, route_ids.shape[0]) - first_slot
    return (route_ids * ways + way_id) * capacity + within


def placement(route_ids, count_tables, capacity):
    ways, tokens = route_ids.shape
    experts = count_tables.shape[1]
    slots = jnp.concatenate(
        [slot_table(route_ids[w], count_tables[w], capacity, w, ways) for w in range(ways)]
    )
    rows = lax.iota(jnp.int32, ways * experts * capacity)
    return (rows[:, None] == slots[None, :]).astype(jnp.bfloat16)


def exchange(blocks, ways):
    experts, rows, model_width = blocks.shape
    capacity = rows // ways
    arrived = lax.all_to_all(blocks, "expert", split_axis=0, concat_axis=0, tiled=True)
    return [
        arrived[:, way_id * capacity:(way_id + 1) * capacity].reshape(experts * capacity, model_width)
        for way_id in range(ways)
    ]


def batched(left, right, contract_left, contract_right):
    return lax.dot_general(
        left, right, (((contract_left,), (contract_right,)), ((0,), (0,))),
        preferred_element_type=jnp.float32,
    )


def expert_grads(slope_rows, saved_rows, weight_in, weight_out):
    hidden_width = weight_out.shape[0]
    gate_up = jnp.dot(saved_rows, weight_in, preferred_element_type=jnp.float32)
    gate_part = gate_up[:, :hidden_width]
    upward = gate_up[:, hidden_width:]
    sigmoid_gate = jax.nn.sigmoid(gate_part)
    active = gate_part * sigmoid_gate
    hidden = (active * upward).astype(jnp.bfloat16)
    hidden_grad = right_product(slope_rows, weight_out)
    gate_grad = hidden_grad * upward * sigmoid_gate * (1.0 + gate_part * (1.0 - sigmoid_gate))
    pair_grad = jnp.concatenate([gate_grad, hidden_grad * active], axis=1).astype(jnp.bfloat16)
    return hidden, pair_grad


def weight_terms(saved_rows, slope_rows, hidden, pair_grad):
    return left_product(saved_rows, pair_grad), left_product(hidden, slope_rows)


def on_device(w_in, w_out, grads, fresh, saved, probs, routes, counts):
    sections = lax.axis_size("section")
    section_id = lax.axis_index("section")
    experts = lax.axis_size("expert")
    model_width = grads.shape[-1]
    tokens = grads.shape[2]
    capacity = 2 * tokens // experts
    hidden_width = w_out.shape[-2]
    ticks = saved.shape[0]
    saved_mirror = mirrored(saved[:, 1, 0, 0], "section")
    current = grads[:, 0]
    zeros_in = jnp.zeros((model_width, 2 * hidden_width), jnp.float32)
    zeros_out = jnp.zeros((hidden_width, model_width), jnp.float32)
    own_in, own_out = zeros_in, zeros_out
    mirror_in, mirror_out = zeros_in, zeros_out
    slope_mirror = None
    for tick_id in range(ticks):
        one_hot = placement(routes[tick_id, :, 0], counts[tick_id, :, 0, 0], capacity)
        scaled = (probs[tick_id, :, 0][:, :, None] * current.astype(jnp.float32)).astype(jnp.bfloat16)
        blocks = jnp.dot(one_hot, scaled.reshape(-1, model_width), preferred_element_type=jnp.float32)
        blocks = blocks.astype(jnp.bfloat16).reshape(experts, 2 * capacity, model_width)
        if slope_mirror is not None:
            hidden_m, pair_grad_m = expert_grads(
                slope_mirror, saved_mirror[tick_id - 1], w_in[0, 0, 0], w_out[0, 0, 0]
            )
            part_in, part_out = weight_terms(
                saved_mirror[tick_id - 1], slope_mirror, hidden_m, pair_grad_m
            )
            mirror_in = mirror_in + part_in
            mirror_out = mirror_out + part_out
        arrived = lax.all_to_all(blocks, "expert", split_axis=0, concat_axis=0, tiled=True)
        slopes = (
            arrived.reshape(experts, 2, capacity, model_width)
            .transpose(1, 0, 2, 3)
            .reshape(2, experts * capacity, model_width)
        )
        saved_rows = saved[tick_id, :, 0, 0]
        gate_up = batched(saved_rows, w_in[:, 0, 0], 2, 1)
        gate_part = gate_up[..., :hidden_width]
        upward = gate_up[..., hidden_width:]
        sigmoid_gate = jax.nn.sigmoid(gate_part)
        active = gate_part * sigmoid_gate
        hidden = (active * upward).astype(jnp.bfloat16)
        hidden_grad = batched(slopes, w_out[:, 0, 0], 2, 2)
        gate_grad = hidden_grad * upward * sigmoid_gate * (1.0 + gate_part * (1.0 - sigmoid_gate))
        pair_grad = jnp.concatenate([gate_grad, hidden_grad * active], axis=2).astype(jnp.bfloat16)
        input_grads = batched(pair_grad, w_in[:, 0, 0], 2, 2).astype(jnp.bfloat16)
        part_in, part_out = weight_terms(saved_rows[0], slopes[0], hidden[0], pair_grad[0])
        own_in = own_in + part_in
        own_out = own_out + part_out
        slope_mirror = mirrored(slopes[1], "section")
        back_blocks = (
            input_grads.reshape(2, experts, capacity, model_width)
            .transpose(1, 0, 2, 3)
            .reshape(experts, 2 * capacity, model_width)
        )
        if tick_id == 0:
            back_blocks, saved_mirror = lax.optimization_barrier((back_blocks, saved_mirror))
        returned = lax.all_to_all(back_blocks, "expert", split_axis=0, concat_axis=0, tiled=True)
        if tick_id + 1 < ticks:
            returned, slope_mirror = lax.optimization_barrier((returned, slope_mirror))
        back_rows = left_product(one_hot, returned.reshape(-1, model_width))
        finished = (current.astype(jnp.float32) + back_rows.reshape(2, tokens, model_width)).astype(
            jnp.bfloat16
        )
        if tick_id + 1 < ticks:
            from_above = passed_along(finished[0], "section", -1)
            from_below = passed_along(finished[1], "section", 1)
            current = jnp.stack([
                jnp.where(section_id == sections - 1, fresh[tick_id, 0], from_above),
                jnp.where(section_id == 0, fresh[tick_id, 1], from_below),
            ])
    hidden_m, pair_grad_m = expert_grads(
        slope_mirror, saved_mirror[ticks - 1], w_in[0, 0, 0], w_out[0, 0, 0]
    )
    part_in, part_out = weight_terms(saved_mirror[ticks - 1], slope_mirror, hidden_m, pair_grad_m)
    mirror_in = (mirror_in + part_in).astype(jnp.bfloat16).astype(jnp.float32)
    mirror_out = (mirror_out + part_out).astype(jnp.bfloat16).astype(jnp.float32)
    grad_in = (own_in + mirror_in).astype(jnp.bfloat16)
    grad_out = (own_out + mirror_out).astype(jnp.bfloat16)
    return (finished[:, None], grad_in[None, None], grad_out[None, None])


def solution(mesh):
    return jax.shard_map(
        on_device,
        mesh=mesh,
        in_specs=(
            P(None, "section", "expert", None, None),
            P(None, "section", "expert", None, None),
            P(None, "section", "expert", None),
            P(None, None, "expert", None),
            P(None, None, "section", "expert", None, None),
            P(None, None, "section", "expert"),
            P(None, None, "section", "expert"),
            P(None, None, "section", "expert", None),
        ),
        out_specs=(
            P(None, "section", "expert", None),
            P("section", "expert", None, None),
            P("section", "expert", None, None),
        ),
        check_vma=False,
    )
```

```python
import jax
import jax.numpy as jnp
from jax import lax
from jax.experimental import pallas as pl
from jax.sharding import PartitionSpec as P


def passed_along(block, axis, distance):
    devices = range(lax.axis_size(axis))
    route = [(i - distance, i) for i in devices if i - distance in devices]
    return lax.ppermute(block, axis, route)


def mirrored(block, axis):
    count = lax.axis_size(axis)
    return lax.ppermute(block, axis, [(i, count - 1 - i) for i in range(count)])


def left_product(left, right):
    return lax.dot_general(
        left, right, (((0,), (0,)), ((), ())), preferred_element_type=jnp.float32
    )


def right_product(left, right):
    return lax.dot_general(
        left, right, (((1,), (1,)), ((), ())), preferred_element_type=jnp.float32
    )


def slot_table(route_ids, count_table, capacity, way_id, ways):
    experts = count_table.shape[0]
    labels = lax.iota(jnp.int32, experts)
    below = jnp.sum(
        jnp.where(labels[None, :] < labels[:, None], count_table[None, :], 0), axis=1
    )
    first_slot = jnp.sum(jnp.where(route_ids[:, None] == labels[None, :], below[None, :], 0), axis=1)
    within = lax.iota(jnp.int32, route_ids.shape[0]) - first_slot
    return (route_ids * ways + way_id) * capacity + within


def placement(route_ids, count_tables, capacity):
    ways, tokens = route_ids.shape
    experts = count_tables.shape[1]
    slots = jnp.concatenate(
        [slot_table(route_ids[w], count_tables[w], capacity, w, ways) for w in range(ways)]
    )
    rows = lax.iota(jnp.int32, ways * experts * capacity)
    return (rows[:, None] == slots[None, :]).astype(jnp.bfloat16)


def expert_grads(slope_rows, saved_rows, weight_in, weight_out):
    hidden_width = weight_out.shape[0]
    gate_up = jnp.dot(saved_rows, weight_in, preferred_element_type=jnp.float32)
    gate_part = gate_up[:, :hidden_width]
    upward = gate_up[:, hidden_width:]
    sigmoid_gate = jax.nn.sigmoid(gate_part)
    active = gate_part * sigmoid_gate
    hidden = (active * upward).astype(jnp.bfloat16)
    hidden_grad = right_product(slope_rows, weight_out)
    gate_grad = hidden_grad * upward * sigmoid_gate * (1.0 + gate_part * (1.0 - sigmoid_gate))
    pair_grad = jnp.concatenate([gate_grad, hidden_grad * active], axis=1).astype(jnp.bfloat16)
    return hidden, pair_grad


def critical_kernel(slope_ref, factor_ref, active_ref, w_out_ref, w_in_ref, input_ref, pair_ref):
    experts, _, capacity, width = slope_ref.shape
    hidden = factor_ref.shape[-1]
    slope = slope_ref[...].astype(jnp.float32).reshape(experts * capacity, width).astype(jnp.bfloat16)
    hidden_grad = lax.dot_general(
        slope, w_out_ref[0], (((1,), (1,)), ((), ())), preferred_element_type=jnp.float32
    )
    gate_grad = (hidden_grad * factor_ref[0]).astype(jnp.bfloat16)
    up_grad = (hidden_grad * active_ref[0]).astype(jnp.bfloat16)
    pair_ref[0, :, :hidden] = gate_grad
    pair_ref[0, :, hidden:] = up_grad
    w_in = w_in_ref[0]
    input_grad = lax.dot_general(
        gate_grad, w_in[:, :hidden], (((1,), (1,)), ((), ())), preferred_element_type=jnp.float32
    ) + lax.dot_general(
        up_grad, w_in[:, hidden:], (((1,), (1,)), ((), ())), preferred_element_type=jnp.float32
    )
    input_ref[...] = input_grad.reshape(experts, 1, capacity, width).astype(input_ref.dtype)


def critical(arrived, factor, active, weight_out, weight_in):
    experts, ways, capacity, width = arrived.shape
    rows, hidden = factor.shape[1], factor.shape[2]
    row_block = pl.BlockSpec((experts, 1, capacity, width), lambda w: (0, w, 0, 0))
    return pl.pallas_call(
        critical_kernel,
        grid=(ways,),
        in_specs=[
            row_block,
            pl.BlockSpec((1, rows, hidden), lambda w: (w, 0, 0)),
            pl.BlockSpec((1, rows, hidden), lambda w: (w, 0, 0)),
            pl.BlockSpec((1,) + weight_out.shape[1:], lambda w: (w, 0, 0)),
            pl.BlockSpec((1,) + weight_in.shape[1:], lambda w: (w, 0, 0)),
        ],
        out_specs=[row_block, pl.BlockSpec((1, rows, 2 * hidden), lambda w: (w, 0, 0))],
        out_shape=[
            jax.ShapeDtypeStruct(arrived.shape, jnp.bfloat16),
            jax.ShapeDtypeStruct((ways, rows, 2 * hidden), jnp.bfloat16),
        ],
        cost_estimate=pl.CostEstimate(
            flops=2 * ways * rows * width * 3 * hidden,
            bytes_accessed=2 * arrived.size * 2 + weight_in.size * 2 + weight_out.size * 2
            + factor.size * 8 + ways * rows * 2 * hidden * 2,
            transcendentals=0,
        ),
    )(arrived, factor, active, weight_out, weight_in)


def gate_terms(saved_rows, weight_in, hidden_width):
    gate_up = lax.dot_general(
        saved_rows, weight_in, (((2,), (1,)), ((0,), (0,))), preferred_element_type=jnp.float32
    )
    gate_part = gate_up[..., :hidden_width]
    upward = gate_up[..., hidden_width:]
    sigmoid_gate = jax.nn.sigmoid(gate_part)
    active = gate_part * sigmoid_gate
    hidden = (active * upward).astype(jnp.bfloat16)
    factor = upward * sigmoid_gate * (1.0 + gate_part * (1.0 - sigmoid_gate))
    return factor, active, hidden


def weight_terms(saved_rows, slope_rows, hidden, pair_grad):
    return left_product(saved_rows, pair_grad), left_product(hidden, slope_rows)


def on_device(w_in, w_out, grads, fresh, saved, probs, routes, counts):
    sections = lax.axis_size("section")
    section_id = lax.axis_index("section")
    experts = lax.axis_size("expert")
    model_width = grads.shape[-1]
    tokens = grads.shape[2]
    capacity = 2 * tokens // experts
    hidden_width = w_out.shape[-2]
    ticks = saved.shape[0]
    saved_mirror = mirrored(saved[:, 1, 0, 0], "section")
    current = grads[:, 0]
    zeros_in = jnp.zeros((model_width, 2 * hidden_width), jnp.float32)
    zeros_out = jnp.zeros((hidden_width, model_width), jnp.float32)
    own_in, own_out = zeros_in, zeros_out
    mirror_in, mirror_out = zeros_in, zeros_out
    slope_mirror = None
    for tick_id in range(ticks):
        one_hot = placement(routes[tick_id, :, 0], counts[tick_id, :, 0, 0], capacity)
        scaled = (probs[tick_id, :, 0][:, :, None] * current.astype(jnp.float32)).astype(jnp.bfloat16)
        blocks = jnp.dot(one_hot, scaled.reshape(-1, model_width), preferred_element_type=jnp.float32)
        blocks = blocks.astype(jnp.bfloat16).reshape(experts, 2, capacity, model_width)
        if slope_mirror is not None:
            hidden_m, pair_grad_m = expert_grads(
                slope_mirror, saved_mirror[tick_id - 1], w_in[0, 0, 0], w_out[0, 0, 0]
            )
            part_in, part_out = weight_terms(
                saved_mirror[tick_id - 1], slope_mirror, hidden_m, pair_grad_m
            )
            mirror_in = mirror_in + part_in
            mirror_out = mirror_out + part_out
        arrived = lax.all_to_all(blocks, "expert", split_axis=0, concat_axis=0, tiled=True)
        factor, active, hidden = gate_terms(saved[tick_id, :, 0, 0], w_in[:, 0, 0], hidden_width)
        back_blocks, pair_grad = critical(arrived, factor, active, w_out[:, 0, 0], w_in[:, 0, 0])
        slopes = [arrived[:, way_id].reshape(experts * capacity, model_width) for way_id in range(2)]
        part_in, part_out = weight_terms(saved[tick_id, 0, 0, 0], slopes[0], hidden[0], pair_grad[0])
        own_in = own_in + part_in
        own_out = own_out + part_out
        slope_mirror = mirrored(slopes[1], "section")
        if tick_id == 0:
            back_blocks, saved_mirror = lax.optimization_barrier((back_blocks, saved_mirror))
        returned = lax.all_to_all(back_blocks, "expert", split_axis=0, concat_axis=0, tiled=True)
        if tick_id + 1 < ticks:
            returned, slope_mirror = lax.optimization_barrier((returned, slope_mirror))
        back_rows = left_product(one_hot, returned.reshape(-1, model_width))
        finished = (current.astype(jnp.float32) + back_rows.reshape(2, tokens, model_width)).astype(
            jnp.bfloat16
        )
        if tick_id + 1 < ticks:
            from_above = passed_along(finished[0], "section", -1)
            from_below = passed_along(finished[1], "section", 1)
            current = jnp.stack([
                jnp.where(section_id == sections - 1, fresh[tick_id, 0], from_above),
                jnp.where(section_id == 0, fresh[tick_id, 1], from_below),
            ])
    hidden_m, pair_grad_m = expert_grads(
        slope_mirror, saved_mirror[ticks - 1], w_in[0, 0, 0], w_out[0, 0, 0]
    )
    part_in, part_out = weight_terms(saved_mirror[ticks - 1], slope_mirror, hidden_m, pair_grad_m)
    mirror_in = (mirror_in + part_in).astype(jnp.bfloat16).astype(jnp.float32)
    mirror_out = (mirror_out + part_out).astype(jnp.bfloat16).astype(jnp.float32)
    grad_in = (own_in + mirror_in).astype(jnp.bfloat16)
    grad_out = (own_out + mirror_out).astype(jnp.bfloat16)
    return (finished[:, None], grad_in[None, None], grad_out[None, None])


def solution(mesh):
    return jax.shard_map(
        on_device,
        mesh=mesh,
        in_specs=(
            P(None, "section", "expert", None, None),
            P(None, "section", "expert", None, None),
            P(None, "section", "expert", None),
            P(None, None, "expert", None),
            P(None, None, "section", "expert", None, None),
            P(None, None, "section", "expert"),
            P(None, None, "section", "expert"),
            P(None, None, "section", "expert", None),
        ),
        out_specs=(
            P(None, "section", "expert", None),
            P("section", "expert", None, None),
            P("section", "expert", None, None),
        ),
        check_vma=False,
    )
```

```python
import jax
import jax.numpy as jnp
from jax import lax
from jax.sharding import PartitionSpec as P


def passed_along(block, axis, distance):
    devices = range(lax.axis_size(axis))
    route = [(i - distance, i) for i in devices if i - distance in devices]
    return lax.ppermute(block, axis, route)


def mirrored(block, axis):
    count = lax.axis_size(axis)
    return lax.ppermute(block, axis, [(i, count - 1 - i) for i in range(count)])


def left_product(left, right):
    return lax.dot_general(
        left, right, (((0,), (0,)), ((), ())), preferred_element_type=jnp.float32
    )


def right_product(left, right):
    return lax.dot_general(
        left, right, (((1,), (1,)), ((), ())), preferred_element_type=jnp.float32
    )


def slot_table(route_ids, count_table, capacity, way_id, ways):
    experts = count_table.shape[0]
    labels = lax.iota(jnp.int32, experts)
    below = jnp.sum(
        jnp.where(labels[None, :] < labels[:, None], count_table[None, :], 0), axis=1
    )
    first_slot = jnp.sum(jnp.where(route_ids[:, None] == labels[None, :], below[None, :], 0), axis=1)
    within = lax.iota(jnp.int32, route_ids.shape[0]) - first_slot
    return (route_ids * ways + way_id) * capacity + within


def placement(route_ids, count_tables, capacity):
    ways, tokens = route_ids.shape
    experts = count_tables.shape[1]
    slots = jnp.concatenate(
        [slot_table(route_ids[w], count_tables[w], capacity, w, ways) for w in range(ways)]
    )
    rows = lax.iota(jnp.int32, ways * experts * capacity)
    return (rows[:, None] == slots[None, :]).astype(jnp.bfloat16)


def exchange(blocks):
    experts, ways, capacity, model_width = blocks.shape
    arrived = lax.all_to_all(blocks, "expert", split_axis=0, concat_axis=0, tiled=True)
    return [arrived[:, way_id].reshape(experts * capacity, model_width) for way_id in range(ways)]


def expert_grads(slope_rows, saved_rows, weight_in, weight_out):
    hidden_width = weight_out.shape[0]
    gate_up = jnp.dot(saved_rows, weight_in, preferred_element_type=jnp.float32)
    gate_part = gate_up[:, :hidden_width]
    upward = gate_up[:, hidden_width:]
    sigmoid_gate = jax.nn.sigmoid(gate_part)
    active = gate_part * sigmoid_gate
    hidden = (active * upward).astype(jnp.bfloat16)
    hidden_grad = right_product(slope_rows, weight_out)
    gate_grad = hidden_grad * upward * sigmoid_gate * (1.0 + gate_part * (1.0 - sigmoid_gate))
    pair_grad = jnp.concatenate([gate_grad, hidden_grad * active], axis=1).astype(jnp.bfloat16)
    return hidden, pair_grad


def weight_terms(saved_rows, slope_rows, hidden, pair_grad):
    return left_product(saved_rows, pair_grad), left_product(hidden, slope_rows)


def on_device(w_in, w_out, grads, fresh, saved, probs, routes, counts):
    sections = lax.axis_size("section")
    section_id = lax.axis_index("section")
    experts = lax.axis_size("expert")
    model_width = grads.shape[-1]
    tokens = grads.shape[2]
    capacity = 2 * tokens // experts
    hidden_width = w_out.shape[-2]
    ticks = saved.shape[0]
    saved_mirror = [mirrored(saved[tick_id, 1, 0, 0], "section") for tick_id in range(saved.shape[0])]
    current = grads[:, 0]
    zeros_in = jnp.zeros((model_width, 2 * hidden_width), jnp.float32)
    zeros_out = jnp.zeros((hidden_width, model_width), jnp.float32)
    own_in, own_out = zeros_in, zeros_out
    mirror_in, mirror_out = zeros_in, zeros_out
    slope_mirror = None
    for tick_id in range(ticks):
        one_hot = placement(routes[tick_id, :, 0], counts[tick_id, :, 0, 0], capacity)
        scaled = (probs[tick_id, :, 0][:, :, None] * current.astype(jnp.float32)).astype(jnp.bfloat16)
        blocks = jnp.dot(one_hot, scaled.reshape(-1, model_width), preferred_element_type=jnp.float32)
        blocks = blocks.astype(jnp.bfloat16).reshape(experts, 2, capacity, model_width)
        if slope_mirror is not None:
            hidden_m, pair_grad_m = expert_grads(
                slope_mirror, saved_mirror[tick_id - 1], w_in[0, 0, 0], w_out[0, 0, 0]
            )
            part_in, part_out = weight_terms(
                saved_mirror[tick_id - 1], slope_mirror, hidden_m, pair_grad_m
            )
            mirror_in = mirror_in + part_in
            mirror_out = mirror_out + part_out
        slopes = exchange(blocks)
        slopes, saved_mirror[tick_id] = lax.optimization_barrier((slopes, saved_mirror[tick_id]))
        input_grads = []
        for way_id in range(2):
            saved_rows = saved[tick_id, way_id, 0, 0]
            hidden, pair_grad = expert_grads(
                slopes[way_id], saved_rows, w_in[way_id, 0, 0], w_out[way_id, 0, 0]
            )
            input_grad = right_product(pair_grad, w_in[way_id, 0, 0]).astype(jnp.bfloat16)
            input_grads.append(input_grad.reshape(experts, 1, capacity, model_width))
            if way_id == 0:
                part_in, part_out = weight_terms(saved_rows, slopes[0], hidden, pair_grad)
                own_in = own_in + part_in
                own_out = own_out + part_out
        slope_mirror = mirrored(slopes[1], "section")
        back_blocks = jnp.concatenate(input_grads, axis=1)
        returned = lax.all_to_all(back_blocks, "expert", split_axis=0, concat_axis=0, tiled=True)
        if tick_id + 1 < ticks:
            returned, slope_mirror = lax.optimization_barrier((returned, slope_mirror))
        back_rows = left_product(one_hot, returned.reshape(-1, model_width))
        finished = (current.astype(jnp.float32) + back_rows.reshape(2, tokens, model_width)).astype(
            jnp.bfloat16
        )
        if tick_id + 1 < ticks:
            from_above = passed_along(finished[0], "section", -1)
            from_below = passed_along(finished[1], "section", 1)
            current = jnp.stack([
                jnp.where(section_id == sections - 1, fresh[tick_id, 0], from_above),
                jnp.where(section_id == 0, fresh[tick_id, 1], from_below),
            ])
    hidden_m, pair_grad_m = expert_grads(
        slope_mirror, saved_mirror[ticks - 1], w_in[0, 0, 0], w_out[0, 0, 0]
    )
    part_in, part_out = weight_terms(saved_mirror[ticks - 1], slope_mirror, hidden_m, pair_grad_m)
    mirror_in = (mirror_in + part_in).astype(jnp.bfloat16).astype(jnp.float32)
    mirror_out = (mirror_out + part_out).astype(jnp.bfloat16).astype(jnp.float32)
    grad_in = (own_in + mirror_in).astype(jnp.bfloat16)
    grad_out = (own_out + mirror_out).astype(jnp.bfloat16)
    return (finished[:, None], grad_in[None, None], grad_out[None, None])


def solution(mesh):
    return jax.shard_map(
        on_device,
        mesh=mesh,
        in_specs=(
            P(None, "section", "expert", None, None),
            P(None, "section", "expert", None, None),
            P(None, "section", "expert", None),
            P(None, None, "expert", None),
            P(None, None, "section", "expert", None, None),
            P(None, None, "section", "expert"),
            P(None, None, "section", "expert"),
            P(None, None, "section", "expert", None),
        ),
        out_specs=(
            P(None, "section", "expert", None),
            P("section", "expert", None, None),
            P("section", "expert", None, None),
        ),
        check_vma=False,
    )
```

```python
import jax
import jax.numpy as jnp
from jax import lax
from jax.sharding import PartitionSpec as P


def passed_along(block, axis, distance):
    devices = range(lax.axis_size(axis))
    route = [(i - distance, i) for i in devices if i - distance in devices]
    return lax.ppermute(block, axis, route)


def mirrored(block, axis):
    count = lax.axis_size(axis)
    return lax.ppermute(block, axis, [(i, count - 1 - i) for i in range(count)])


def left_product(left, right):
    return lax.dot_general(
        left, right, (((0,), (0,)), ((), ())), preferred_element_type=jnp.float32
    )


def right_product(left, right):
    return lax.dot_general(
        left, right, (((1,), (1,)), ((), ())), preferred_element_type=jnp.float32
    )


def slot_table(route_ids, count_table, capacity, way_id, ways):
    experts = count_table.shape[0]
    labels = lax.iota(jnp.int32, experts)
    below = jnp.sum(
        jnp.where(labels[None, :] < labels[:, None], count_table[None, :], 0), axis=1
    )
    first_slot = jnp.sum(jnp.where(route_ids[:, None] == labels[None, :], below[None, :], 0), axis=1)
    within = lax.iota(jnp.int32, route_ids.shape[0]) - first_slot
    return (route_ids * ways + way_id) * capacity + within


def placement(route_ids, count_tables, capacity):
    ways, tokens = route_ids.shape
    experts = count_tables.shape[1]
    slots = jnp.concatenate(
        [slot_table(route_ids[w], count_tables[w], capacity, w, ways) for w in range(ways)]
    )
    rows = lax.iota(jnp.int32, ways * experts * capacity)
    return (rows[:, None] == slots[None, :]).astype(jnp.bfloat16)


def exchange(blocks):
    experts, ways, capacity, model_width = blocks.shape
    arrived = lax.all_to_all(blocks, "expert", split_axis=0, concat_axis=0, tiled=True)
    return [arrived[:, way_id].reshape(experts * capacity, model_width) for way_id in range(ways)]


def expert_grads(slope_rows, saved_rows, weight_in, weight_out):
    hidden_width = weight_out.shape[0]
    gate_up = jnp.dot(saved_rows, weight_in, preferred_element_type=jnp.float32)
    gate_part = gate_up[:, :hidden_width]
    upward = gate_up[:, hidden_width:]
    sigmoid_gate = jax.nn.sigmoid(gate_part)
    active = gate_part * sigmoid_gate
    hidden = (active * upward).astype(jnp.bfloat16)
    hidden_grad = right_product(slope_rows, weight_out)
    gate_grad = hidden_grad * upward * sigmoid_gate * (1.0 + gate_part * (1.0 - sigmoid_gate))
    pair_grad = jnp.concatenate([gate_grad, hidden_grad * active], axis=1).astype(jnp.bfloat16)
    return hidden, pair_grad


def weight_terms(saved_rows, slope_rows, hidden, pair_grad):
    return left_product(saved_rows, pair_grad), left_product(hidden, slope_rows)


def on_device(w_in, w_out, grads, fresh, saved, probs, routes, counts):
    sections = lax.axis_size("section")
    section_id = lax.axis_index("section")
    experts = lax.axis_size("expert")
    model_width = grads.shape[-1]
    tokens = grads.shape[2]
    capacity = 2 * tokens // experts
    hidden_width = w_out.shape[-2]
    ticks = saved.shape[0]
    saved_mirror = [mirrored(saved[tick_id, 1, 0, 0], "section") for tick_id in range(saved.shape[0])]
    current = grads[:, 0]
    zeros_in = jnp.zeros((model_width, 2 * hidden_width), jnp.float32)
    zeros_out = jnp.zeros((hidden_width, model_width), jnp.float32)
    own_in, own_out = zeros_in, zeros_out
    mirror_in, mirror_out = zeros_in, zeros_out
    slope_mirror = None
    for tick_id in range(ticks):
        one_hot = placement(routes[tick_id, :, 0], counts[tick_id, :, 0, 0], capacity)
        scaled = (probs[tick_id, :, 0][:, :, None] * current.astype(jnp.float32)).astype(jnp.bfloat16)
        blocks = jnp.dot(one_hot, scaled.reshape(-1, model_width), preferred_element_type=jnp.float32)
        blocks = blocks.astype(jnp.bfloat16).reshape(experts, 2, capacity, model_width)
        blocks, tick_w_in, tick_w_out = lax.optimization_barrier((blocks, w_in[:, 0, 0], w_out[:, 0, 0]))
        if slope_mirror is not None:
            hidden_m, pair_grad_m = expert_grads(
                slope_mirror, saved_mirror[tick_id - 1], w_in[0, 0, 0], w_out[0, 0, 0]
            )
            part_in, part_out = weight_terms(
                saved_mirror[tick_id - 1], slope_mirror, hidden_m, pair_grad_m
            )
            mirror_in = mirror_in + part_in
            mirror_out = mirror_out + part_out
        slopes = exchange(blocks)
        slopes, saved_mirror[tick_id] = lax.optimization_barrier((slopes, saved_mirror[tick_id]))
        input_grads = []
        for way_id in range(2):
            saved_rows = saved[tick_id, way_id, 0, 0]
            hidden, pair_grad = expert_grads(
                slopes[way_id], saved_rows, tick_w_in[way_id], tick_w_out[way_id]
            )
            input_grad = right_product(pair_grad, tick_w_in[way_id]).astype(jnp.bfloat16)
            input_grads.append(input_grad.reshape(experts, 1, capacity, model_width))
            if way_id == 0:
                part_in, part_out = weight_terms(saved_rows, slopes[0], hidden, pair_grad)
                own_in = own_in + part_in
                own_out = own_out + part_out
        slope_mirror = mirrored(slopes[1], "section")
        back_blocks = jnp.concatenate(input_grads, axis=1)
        returned = lax.all_to_all(back_blocks, "expert", split_axis=0, concat_axis=0, tiled=True)
        if tick_id + 1 < ticks:
            returned, slope_mirror = lax.optimization_barrier((returned, slope_mirror))
        back_rows = left_product(one_hot, returned.reshape(-1, model_width))
        finished = (current.astype(jnp.float32) + back_rows.reshape(2, tokens, model_width)).astype(
            jnp.bfloat16
        )
        if tick_id + 1 < ticks:
            from_above = passed_along(finished[0], "section", -1)
            from_below = passed_along(finished[1], "section", 1)
            current = jnp.stack([
                jnp.where(section_id == sections - 1, fresh[tick_id, 0], from_above),
                jnp.where(section_id == 0, fresh[tick_id, 1], from_below),
            ])
    hidden_m, pair_grad_m = expert_grads(
        slope_mirror, saved_mirror[ticks - 1], w_in[0, 0, 0], w_out[0, 0, 0]
    )
    part_in, part_out = weight_terms(saved_mirror[ticks - 1], slope_mirror, hidden_m, pair_grad_m)
    mirror_in = (mirror_in + part_in).astype(jnp.bfloat16).astype(jnp.float32)
    mirror_out = (mirror_out + part_out).astype(jnp.bfloat16).astype(jnp.float32)
    grad_in = (own_in + mirror_in).astype(jnp.bfloat16)
    grad_out = (own_out + mirror_out).astype(jnp.bfloat16)
    return (finished[:, None], grad_in[None, None], grad_out[None, None])


def solution(mesh):
    return jax.shard_map(
        on_device,
        mesh=mesh,
        in_specs=(
            P(None, "section", "expert", None, None),
            P(None, "section", "expert", None, None),
            P(None, "section", "expert", None),
            P(None, None, "expert", None),
            P(None, None, "section", "expert", None, None),
            P(None, None, "section", "expert"),
            P(None, None, "section", "expert"),
            P(None, None, "section", "expert", None),
        ),
        out_specs=(
            P(None, "section", "expert", None),
            P("section", "expert", None, None),
            P("section", "expert", None, None),
        ),
        check_vma=False,
    )
```

```python
import jax
import jax.numpy as jnp
from jax import lax
from jax.sharding import PartitionSpec as P


def passed_along(block, axis, distance):
    devices = range(lax.axis_size(axis))
    route = [(i - distance, i) for i in devices if i - distance in devices]
    return lax.ppermute(block, axis, route)


def mirrored(block, axis):
    count = lax.axis_size(axis)
    return lax.ppermute(block, axis, [(i, count - 1 - i) for i in range(count)])


def left_product(left, right):
    return lax.dot_general(
        left, right, (((0,), (0,)), ((), ())), preferred_element_type=jnp.float32
    )


def right_product(left, right):
    return lax.dot_general(
        left, right, (((1,), (1,)), ((), ())), preferred_element_type=jnp.float32
    )


def slot_table(route_ids, count_table, capacity, way_id, ways):
    experts = count_table.shape[0]
    labels = lax.iota(jnp.int32, experts)
    below = jnp.sum(
        jnp.where(labels[None, :] < labels[:, None], count_table[None, :], 0), axis=1
    )
    first_slot = jnp.sum(jnp.where(route_ids[:, None] == labels[None, :], below[None, :], 0), axis=1)
    within = lax.iota(jnp.int32, route_ids.shape[0]) - first_slot
    return (route_ids * ways + way_id) * capacity + within


def placement(route_ids, count_tables, capacity):
    ways, tokens = route_ids.shape
    experts = count_tables.shape[1]
    slots = jnp.concatenate(
        [slot_table(route_ids[w], count_tables[w], capacity, w, ways) for w in range(ways)]
    )
    rows = lax.iota(jnp.int32, ways * experts * capacity)
    return (rows[:, None] == slots[None, :]).astype(jnp.bfloat16)


def exchange(blocks):
    experts, ways, capacity, model_width = blocks.shape
    arrived = lax.all_to_all(blocks, "expert", split_axis=0, concat_axis=0, tiled=True)
    return [arrived[:, way_id].reshape(experts * capacity, model_width) for way_id in range(ways)]


def expert_grads(slope_rows, saved_rows, weight_in, weight_out):
    hidden_width = weight_out.shape[0]
    gate_up = jnp.dot(saved_rows, weight_in, preferred_element_type=jnp.float32)
    gate_part = gate_up[:, :hidden_width]
    upward = gate_up[:, hidden_width:]
    sigmoid_gate = jax.nn.sigmoid(gate_part)
    active = gate_part * sigmoid_gate
    hidden = (active * upward).astype(jnp.bfloat16)
    hidden_grad = right_product(slope_rows, weight_out)
    gate_grad = hidden_grad * upward * sigmoid_gate * (1.0 + gate_part * (1.0 - sigmoid_gate))
    pair_grad = jnp.concatenate([gate_grad, hidden_grad * active], axis=1).astype(jnp.bfloat16)
    return hidden, pair_grad


def weight_terms(saved_rows, slope_rows, hidden, pair_grad):
    return left_product(saved_rows, pair_grad), left_product(hidden, slope_rows)


def on_device(w_in, w_out, grads, fresh, saved, probs, routes, counts):
    sections = lax.axis_size("section")
    section_id = lax.axis_index("section")
    experts = lax.axis_size("expert")
    model_width = grads.shape[-1]
    tokens = grads.shape[2]
    capacity = 2 * tokens // experts
    hidden_width = w_out.shape[-2]
    ticks = saved.shape[0]
    saved_mirror = mirrored(saved[:, 1, 0, 0], "section")
    current = grads[:, 0]
    zeros_in = jnp.zeros((model_width, 2 * hidden_width), jnp.float32)
    zeros_out = jnp.zeros((hidden_width, model_width), jnp.float32)
    own_in, own_out = zeros_in, zeros_out
    mirror_in, mirror_out = zeros_in, zeros_out
    slope_mirror = None
    for tick_id in range(ticks):
        one_hot = placement(routes[tick_id, :, 0], counts[tick_id, :, 0, 0], capacity)
        scaled = (probs[tick_id, :, 0][:, :, None] * current.astype(jnp.float32)).astype(jnp.bfloat16)
        scaled = lax.optimization_barrier(scaled)
        blocks = jnp.dot(one_hot, scaled.reshape(-1, model_width), preferred_element_type=jnp.float32)
        blocks = blocks.astype(jnp.bfloat16).reshape(experts, 2, capacity, model_width)
        if slope_mirror is not None:
            hidden_m, pair_grad_m = expert_grads(
                slope_mirror, saved_mirror[tick_id - 1], w_in[0, 0, 0], w_out[0, 0, 0]
            )
            part_in, part_out = weight_terms(
                saved_mirror[tick_id - 1], slope_mirror, hidden_m, pair_grad_m
            )
            mirror_in = mirror_in + part_in
            mirror_out = mirror_out + part_out
        slopes = exchange(blocks)
        input_grads = []
        for way_id in range(2):
            saved_rows = saved[tick_id, way_id, 0, 0]
            hidden, pair_grad = expert_grads(
                slopes[way_id], saved_rows, w_in[way_id, 0, 0], w_out[way_id, 0, 0]
            )
            input_grad = right_product(pair_grad, w_in[way_id, 0, 0]).astype(jnp.bfloat16)
            input_grads.append(input_grad.reshape(experts, 1, capacity, model_width))
            if way_id == 0:
                part_in, part_out = weight_terms(saved_rows, slopes[0], hidden, pair_grad)
                own_in = own_in + part_in
                own_out = own_out + part_out
        slope_mirror = mirrored(slopes[1], "section")
        back_blocks = jnp.concatenate(input_grads, axis=1)
        if tick_id == 0:
            back_blocks, saved_mirror = lax.optimization_barrier((back_blocks, saved_mirror))
        returned = lax.all_to_all(back_blocks, "expert", split_axis=0, concat_axis=0, tiled=True)
        if tick_id + 1 < ticks:
            returned, slope_mirror = lax.optimization_barrier((returned, slope_mirror))
        back_rows = left_product(one_hot, returned.reshape(-1, model_width))
        finished = (current.astype(jnp.float32) + back_rows.reshape(2, tokens, model_width)).astype(
            jnp.bfloat16
        )
        if tick_id + 1 < ticks:
            from_above = passed_along(finished[0], "section", -1)
            from_below = passed_along(finished[1], "section", 1)
            current = jnp.stack([
                jnp.where(section_id == sections - 1, fresh[tick_id, 0], from_above),
                jnp.where(section_id == 0, fresh[tick_id, 1], from_below),
            ])
    hidden_m, pair_grad_m = expert_grads(
        slope_mirror, saved_mirror[ticks - 1], w_in[0, 0, 0], w_out[0, 0, 0]
    )
    part_in, part_out = weight_terms(saved_mirror[ticks - 1], slope_mirror, hidden_m, pair_grad_m)
    mirror_in = (mirror_in + part_in).astype(jnp.bfloat16).astype(jnp.float32)
    mirror_out = (mirror_out + part_out).astype(jnp.bfloat16).astype(jnp.float32)
    grad_in = (own_in + mirror_in).astype(jnp.bfloat16)
    grad_out = (own_out + mirror_out).astype(jnp.bfloat16)
    return (finished[:, None], grad_in[None, None], grad_out[None, None])


def solution(mesh):
    return jax.shard_map(
        on_device,
        mesh=mesh,
        in_specs=(
            P(None, "section", "expert", None, None),
            P(None, "section", "expert", None, None),
            P(None, "section", "expert", None),
            P(None, None, "expert", None),
            P(None, None, "section", "expert", None, None),
            P(None, None, "section", "expert"),
            P(None, None, "section", "expert"),
            P(None, None, "section", "expert", None),
        ),
        out_specs=(
            P(None, "section", "expert", None),
            P("section", "expert", None, None),
            P("section", "expert", None, None),
        ),
        check_vma=False,
    )
```

```python
import jax
import jax.numpy as jnp
from jax import lax
from jax.sharding import PartitionSpec as P


def passed_along(block, axis, distance):
    devices = range(lax.axis_size(axis))
    route = [(i - distance, i) for i in devices if i - distance in devices]
    return lax.ppermute(block, axis, route)


def mirrored(block, axis):
    count = lax.axis_size(axis)
    return lax.ppermute(block, axis, [(i, count - 1 - i) for i in range(count)])


def left_product(left, right):
    return lax.dot_general(
        left, right, (((0,), (0,)), ((), ())), preferred_element_type=jnp.float32
    )


def right_product(left, right):
    return lax.dot_general(
        left, right, (((1,), (1,)), ((), ())), preferred_element_type=jnp.float32
    )


def slot_table(route_ids, capacity, way_id, ways):
    tokens = route_ids.shape[0]
    positions = lax.iota(jnp.int32, tokens)
    earlier = (positions[None, :] < positions[:, None]) & (route_ids[None, :] == route_ids[:, None])
    within = jnp.sum(earlier.astype(jnp.int32), axis=1)
    return (route_ids * ways + way_id) * capacity + within


def placement(route_ids, capacity, experts):
    ways, tokens = route_ids.shape
    slots = jnp.concatenate(
        [slot_table(route_ids[w], capacity, w, ways) for w in range(ways)]
    )
    rows = lax.iota(jnp.int32, ways * experts * capacity)
    return (rows[:, None] == slots[None, :]).astype(jnp.bfloat16)


def exchange(blocks):
    experts, ways, capacity, model_width = blocks.shape
    arrived = lax.all_to_all(blocks, "expert", split_axis=0, concat_axis=0, tiled=True)
    return [arrived[:, way_id].reshape(experts * capacity, model_width) for way_id in range(ways)]


def expert_grads(slope_rows, saved_rows, weight_in, weight_out):
    hidden_width = weight_out.shape[0]
    gate_up = jnp.dot(saved_rows, weight_in, preferred_element_type=jnp.float32)
    gate_part = gate_up[:, :hidden_width]
    upward = gate_up[:, hidden_width:]
    sigmoid_gate = jax.nn.sigmoid(gate_part)
    active = gate_part * sigmoid_gate
    hidden = (active * upward).astype(jnp.bfloat16)
    hidden_grad = right_product(slope_rows, weight_out)
    gate_grad = hidden_grad * upward * sigmoid_gate * (1.0 + gate_part * (1.0 - sigmoid_gate))
    pair_grad = jnp.concatenate([gate_grad, hidden_grad * active], axis=1).astype(jnp.bfloat16)
    return hidden, pair_grad


def weight_terms(saved_rows, slope_rows, hidden, pair_grad):
    return left_product(saved_rows, pair_grad), left_product(hidden, slope_rows)


def on_device(w_in, w_out, grads, fresh, saved, probs, routes, counts):
    sections = lax.axis_size("section")
    section_id = lax.axis_index("section")
    experts = lax.axis_size("expert")
    model_width = grads.shape[-1]
    tokens = grads.shape[2]
    capacity = 2 * tokens // experts
    hidden_width = w_out.shape[-2]
    ticks = saved.shape[0]
    saved_mirror = mirrored(saved[:, 1, 0, 0], "section")
    current = grads[:, 0]
    zeros_in = jnp.zeros((model_width, 2 * hidden_width), jnp.float32)
    zeros_out = jnp.zeros((hidden_width, model_width), jnp.float32)
    own_in, own_out = zeros_in, zeros_out
    mirror_in, mirror_out = zeros_in, zeros_out
    slope_mirror = None
    for tick_id in range(ticks):
        one_hot = placement(routes[tick_id, :, 0], capacity, experts)
        scaled = (probs[tick_id, :, 0][:, :, None] * current.astype(jnp.float32)).astype(jnp.bfloat16)
        blocks = jnp.dot(one_hot, scaled.reshape(-1, model_width), preferred_element_type=jnp.float32)
        blocks = blocks.astype(jnp.bfloat16).reshape(experts, 2, capacity, model_width)
        if slope_mirror is not None:
            hidden_m, pair_grad_m = expert_grads(
                slope_mirror, saved_mirror[tick_id - 1], w_in[0, 0, 0], w_out[0, 0, 0]
            )
            part_in, part_out = weight_terms(
                saved_mirror[tick_id - 1], slope_mirror, hidden_m, pair_grad_m
            )
            mirror_in = mirror_in + part_in
            mirror_out = mirror_out + part_out
        slopes = exchange(blocks)
        input_grads = []
        for way_id in range(2):
            saved_rows = saved[tick_id, way_id, 0, 0]
            hidden, pair_grad = expert_grads(
                slopes[way_id], saved_rows, w_in[way_id, 0, 0], w_out[way_id, 0, 0]
            )
            input_grad = right_product(pair_grad, w_in[way_id, 0, 0]).astype(jnp.bfloat16)
            input_grads.append(input_grad.reshape(experts, 1, capacity, model_width))
            if way_id == 0:
                part_in, part_out = weight_terms(saved_rows, slopes[0], hidden, pair_grad)
                own_in = own_in + part_in
                own_out = own_out + part_out
        slope_mirror = mirrored(slopes[1], "section")
        back_blocks = jnp.concatenate(input_grads, axis=1)
        if tick_id == 0:
            back_blocks, saved_mirror = lax.optimization_barrier((back_blocks, saved_mirror))
        returned = lax.all_to_all(back_blocks, "expert", split_axis=0, concat_axis=0, tiled=True)
        if tick_id + 1 < ticks:
            returned, slope_mirror = lax.optimization_barrier((returned, slope_mirror))
        back_rows = left_product(one_hot, returned.reshape(-1, model_width))
        finished = (current.astype(jnp.float32) + back_rows.reshape(2, tokens, model_width)).astype(
            jnp.bfloat16
        )
        if tick_id + 1 < ticks:
            from_above = passed_along(finished[0], "section", -1)
            from_below = passed_along(finished[1], "section", 1)
            current = jnp.stack([
                jnp.where(section_id == sections - 1, fresh[tick_id, 0], from_above),
                jnp.where(section_id == 0, fresh[tick_id, 1], from_below),
            ])
    hidden_m, pair_grad_m = expert_grads(
        slope_mirror, saved_mirror[ticks - 1], w_in[0, 0, 0], w_out[0, 0, 0]
    )
    part_in, part_out = weight_terms(saved_mirror[ticks - 1], slope_mirror, hidden_m, pair_grad_m)
    mirror_in = (mirror_in + part_in).astype(jnp.bfloat16).astype(jnp.float32)
    mirror_out = (mirror_out + part_out).astype(jnp.bfloat16).astype(jnp.float32)
    grad_in = (own_in + mirror_in).astype(jnp.bfloat16)
    grad_out = (own_out + mirror_out).astype(jnp.bfloat16)
    return (finished[:, None], grad_in[None, None], grad_out[None, None])


def solution(mesh):
    return jax.shard_map(
        on_device,
        mesh=mesh,
        in_specs=(
            P(None, "section", "expert", None, None),
            P(None, "section", "expert", None, None),
            P(None, "section", "expert", None),
            P(None, None, "expert", None),
            P(None, None, "section", "expert", None, None),
            P(None, None, "section", "expert"),
            P(None, None, "section", "expert"),
            P(None, None, "section", "expert", None),
        ),
        out_specs=(
            P(None, "section", "expert", None),
            P("section", "expert", None, None),
            P("section", "expert", None, None),
        ),
        check_vma=False,
    )
```

```python
import jax
import jax.numpy as jnp
from jax import lax
from jax.sharding import PartitionSpec as P


def passed_along(block, axis, distance):
    devices = range(lax.axis_size(axis))
    route = [(i - distance, i) for i in devices if i - distance in devices]
    return lax.ppermute(block, axis, route)


def mirrored(block, axis):
    count = lax.axis_size(axis)
    return lax.ppermute(block, axis, [(i, count - 1 - i) for i in range(count)])


def left_product(left, right):
    return lax.dot_general(
        left, right, (((0,), (0,)), ((), ())), preferred_element_type=jnp.float32
    )


def right_product(left, right):
    return lax.dot_general(
        left, right, (((1,), (1,)), ((), ())), preferred_element_type=jnp.float32
    )


def slot_table(route_ids, capacity, way_id, ways):
    tokens = route_ids.shape[0]
    positions = lax.iota(jnp.int32, tokens)
    earlier = (positions[None, :] < positions[:, None]) & (route_ids[None, :] == route_ids[:, None])
    within = jnp.sum(earlier.astype(jnp.int32), axis=1)
    return (route_ids * ways + way_id) * capacity + within


def placement(route_ids, capacity, experts):
    ways, tokens = route_ids.shape
    slots = jnp.concatenate(
        [slot_table(route_ids[w], capacity, w, ways) for w in range(ways)]
    )
    rows = lax.iota(jnp.int32, ways * experts * capacity)
    scatter = (rows[:, None] == slots[None, :]).astype(jnp.bfloat16)
    gather = (slots[:, None] == rows[None, :]).astype(jnp.bfloat16)
    return scatter, gather


def exchange(blocks):
    experts, ways, capacity, model_width = blocks.shape
    arrived = lax.all_to_all(blocks, "expert", split_axis=0, concat_axis=0, tiled=True)
    return [arrived[:, way_id].reshape(experts * capacity, model_width) for way_id in range(ways)]


def expert_grads(slope_rows, saved_rows, weight_in, weight_out):
    hidden_width = weight_out.shape[0]
    gate_up = jnp.dot(saved_rows, weight_in, preferred_element_type=jnp.float32)
    gate_part = gate_up[:, :hidden_width]
    upward = gate_up[:, hidden_width:]
    sigmoid_gate = jax.nn.sigmoid(gate_part)
    active = gate_part * sigmoid_gate
    hidden = (active * upward).astype(jnp.bfloat16)
    hidden_grad = right_product(slope_rows, weight_out)
    gate_grad = hidden_grad * upward * sigmoid_gate * (1.0 + gate_part * (1.0 - sigmoid_gate))
    pair_grad = jnp.concatenate([gate_grad, hidden_grad * active], axis=1).astype(jnp.bfloat16)
    return hidden, pair_grad


def weight_terms(saved_rows, slope_rows, hidden, pair_grad):
    return left_product(saved_rows, pair_grad), left_product(hidden, slope_rows)


def on_device(w_in, w_out, grads, fresh, saved, probs, routes, counts):
    sections = lax.axis_size("section")
    section_id = lax.axis_index("section")
    experts = lax.axis_size("expert")
    model_width = grads.shape[-1]
    tokens = grads.shape[2]
    capacity = 2 * tokens // experts
    hidden_width = w_out.shape[-2]
    ticks = saved.shape[0]
    saved_mirror = mirrored(saved[:, 1, 0, 0], "section")
    current = grads[:, 0]
    zeros_in = jnp.zeros((model_width, 2 * hidden_width), jnp.float32)
    zeros_out = jnp.zeros((hidden_width, model_width), jnp.float32)
    own_in, own_out = zeros_in, zeros_out
    mirror_in, mirror_out = zeros_in, zeros_out
    slope_mirror = None
    for tick_id in range(ticks):
        one_hot, one_hot_back = placement(routes[tick_id, :, 0], capacity, experts)
        scaled = (probs[tick_id, :, 0][:, :, None] * current.astype(jnp.float32)).astype(jnp.bfloat16)
        blocks = jnp.dot(one_hot, scaled.reshape(-1, model_width), preferred_element_type=jnp.float32)
        blocks = blocks.astype(jnp.bfloat16).reshape(experts, 2, capacity, model_width)
        if slope_mirror is not None:
            hidden_m, pair_grad_m = expert_grads(
                slope_mirror, saved_mirror[tick_id - 1], w_in[0, 0, 0], w_out[0, 0, 0]
            )
            part_in, part_out = weight_terms(
                saved_mirror[tick_id - 1], slope_mirror, hidden_m, pair_grad_m
            )
            mirror_in = mirror_in + part_in
            mirror_out = mirror_out + part_out
        slopes = exchange(blocks)
        input_grads = []
        for way_id in range(2):
            saved_rows = saved[tick_id, way_id, 0, 0]
            hidden, pair_grad = expert_grads(
                slopes[way_id], saved_rows, w_in[way_id, 0, 0], w_out[way_id, 0, 0]
            )
            input_grad = right_product(pair_grad, w_in[way_id, 0, 0]).astype(jnp.bfloat16)
            input_grads.append(input_grad.reshape(experts, 1, capacity, model_width))
            if way_id == 0:
                part_in, part_out = weight_terms(saved_rows, slopes[0], hidden, pair_grad)
                own_in = own_in + part_in
                own_out = own_out + part_out
        slope_mirror = mirrored(slopes[1], "section")
        back_blocks = jnp.concatenate(input_grads, axis=1)
        if tick_id == 0:
            back_blocks, saved_mirror = lax.optimization_barrier((back_blocks, saved_mirror))
        returned = lax.all_to_all(back_blocks, "expert", split_axis=0, concat_axis=0, tiled=True)
        if tick_id + 1 < ticks:
            returned, slope_mirror = lax.optimization_barrier((returned, slope_mirror))
        back_rows = jnp.dot(one_hot_back, returned.reshape(-1, model_width), preferred_element_type=jnp.float32)
        finished = (current.astype(jnp.float32) + back_rows.reshape(2, tokens, model_width)).astype(
            jnp.bfloat16
        )
        if tick_id + 1 < ticks:
            from_above = passed_along(finished[0], "section", -1)
            from_below = passed_along(finished[1], "section", 1)
            current = jnp.stack([
                jnp.where(section_id == sections - 1, fresh[tick_id, 0], from_above),
                jnp.where(section_id == 0, fresh[tick_id, 1], from_below),
            ])
    hidden_m, pair_grad_m = expert_grads(
        slope_mirror, saved_mirror[ticks - 1], w_in[0, 0, 0], w_out[0, 0, 0]
    )
    part_in, part_out = weight_terms(saved_mirror[ticks - 1], slope_mirror, hidden_m, pair_grad_m)
    mirror_in = (mirror_in + part_in).astype(jnp.bfloat16).astype(jnp.float32)
    mirror_out = (mirror_out + part_out).astype(jnp.bfloat16).astype(jnp.float32)
    grad_in = (own_in + mirror_in).astype(jnp.bfloat16)
    grad_out = (own_out + mirror_out).astype(jnp.bfloat16)
    return (finished[:, None], grad_in[None, None], grad_out[None, None])


def solution(mesh):
    return jax.shard_map(
        on_device,
        mesh=mesh,
        in_specs=(
            P(None, "section", "expert", None, None),
            P(None, "section", "expert", None, None),
            P(None, "section", "expert", None),
            P(None, None, "expert", None),
            P(None, None, "section", "expert", None, None),
            P(None, None, "section", "expert"),
            P(None, None, "section", "expert"),
            P(None, None, "section", "expert", None),
        ),
        out_specs=(
            P(None, "section", "expert", None),
            P("section", "expert", None, None),
            P("section", "expert", None, None),
        ),
        check_vma=False,
    )
```

```python
import jax
import jax.numpy as jnp
from jax import lax
from jax.sharding import PartitionSpec as P


def passed_along(block, axis, distance):
    devices = range(lax.axis_size(axis))
    route = [(i - distance, i) for i in devices if i - distance in devices]
    return lax.ppermute(block, axis, route)


def mirrored(block, axis):
    count = lax.axis_size(axis)
    return lax.ppermute(block, axis, [(i, count - 1 - i) for i in range(count)])


def left_product(left, right):
    return lax.dot_general(
        left, right, (((0,), (0,)), ((), ())), preferred_element_type=jnp.float32
    )


def right_product(left, right):
    return lax.dot_general(
        left, right, (((1,), (1,)), ((), ())), preferred_element_type=jnp.float32
    )


def slot_table(route_ids, capacity, way_id, ways):
    tokens = route_ids.shape[0]
    positions = lax.iota(jnp.int32, tokens)
    earlier = (positions[None, :] < positions[:, None]) & (route_ids[None, :] == route_ids[:, None])
    within = jnp.sum(earlier.astype(jnp.int32), axis=1)
    return (route_ids * ways + way_id) * capacity + within


def placement(route_ids, capacity, experts):
    ways, tokens = route_ids.shape
    slots = jnp.concatenate(
        [slot_table(route_ids[w], capacity, w, ways) for w in range(ways)]
    )
    rows = lax.iota(jnp.int32, ways * experts * capacity)
    scatter = (rows[:, None] == slots[None, :]).astype(jnp.bfloat16)
    gather = (slots[:, None] == rows[None, :]).astype(jnp.bfloat16)
    return scatter, gather


def exchange(blocks):
    experts, ways, capacity, model_width = blocks.shape
    arrived = lax.all_to_all(blocks, "expert", split_axis=0, concat_axis=0, tiled=True)
    return arrived, [arrived[:, way_id].reshape(experts * capacity, model_width) for way_id in range(ways)]


def expert_grads(slope_rows, saved_rows, weight_in, weight_out):
    hidden_width = weight_out.shape[0]
    gate_up = jnp.dot(saved_rows, weight_in, preferred_element_type=jnp.float32)
    gate_part = gate_up[:, :hidden_width]
    upward = gate_up[:, hidden_width:]
    sigmoid_gate = jax.nn.sigmoid(gate_part)
    active = gate_part * sigmoid_gate
    hidden = (active * upward).astype(jnp.bfloat16)
    hidden_grad = right_product(slope_rows, weight_out)
    gate_grad = hidden_grad * upward * sigmoid_gate * (1.0 + gate_part * (1.0 - sigmoid_gate))
    pair_grad = jnp.concatenate([gate_grad, hidden_grad * active], axis=1).astype(jnp.bfloat16)
    return hidden, pair_grad


def weight_terms(saved_rows, slope_rows, hidden, pair_grad):
    return left_product(saved_rows, pair_grad), left_product(hidden, slope_rows)


def on_device(w_in, w_out, grads, fresh, saved, probs, routes, counts):
    sections = lax.axis_size("section")
    section_id = lax.axis_index("section")
    experts = lax.axis_size("expert")
    model_width = grads.shape[-1]
    tokens = grads.shape[2]
    capacity = 2 * tokens // experts
    hidden_width = w_out.shape[-2]
    ticks = saved.shape[0]
    saved_mirror = mirrored(saved[:, 1, 0, 0], "section")
    current = grads[:, 0]
    zeros_in = jnp.zeros((model_width, 2 * hidden_width), jnp.float32)
    zeros_out = jnp.zeros((hidden_width, model_width), jnp.float32)
    own_in, own_out = zeros_in, zeros_out
    mirror_in, mirror_out = zeros_in, zeros_out
    slope_mirror = None
    for tick_id in range(ticks):
        one_hot, one_hot_back = placement(routes[tick_id, :, 0], capacity, experts)
        scaled = (probs[tick_id, :, 0][:, :, None] * current.astype(jnp.float32)).astype(jnp.bfloat16)
        blocks = jnp.dot(one_hot, scaled.reshape(-1, model_width), preferred_element_type=jnp.float32)
        blocks = blocks.astype(jnp.bfloat16).reshape(experts, 2, capacity, model_width)
        if slope_mirror is not None:
            hidden_m, pair_grad_m = expert_grads(
                slope_mirror, saved_mirror[tick_id - 1], w_in[0, 0, 0], w_out[0, 0, 0]
            )
            part_in, part_out = weight_terms(
                saved_mirror[tick_id - 1], slope_mirror, hidden_m, pair_grad_m
            )
            mirror_in = mirror_in + part_in
            mirror_out = mirror_out + part_out
        arrived, slopes = exchange(blocks)
        input_grads = []
        for way_id in range(2):
            saved_rows = saved[tick_id, way_id, 0, 0]
            hidden, pair_grad = expert_grads(
                slopes[way_id], saved_rows, w_in[way_id, 0, 0], w_out[way_id, 0, 0]
            )
            input_grad = right_product(pair_grad, w_in[way_id, 0, 0]).astype(jnp.bfloat16)
            input_grads.append(input_grad.reshape(experts, 1, capacity, model_width))
            if way_id == 0:
                part_in, part_out = weight_terms(saved_rows, slopes[0], hidden, pair_grad)
                own_in = own_in + part_in
                own_out = own_out + part_out
        back_blocks = jnp.concatenate(input_grads, axis=1)
        back_blocks, arrived = lax.optimization_barrier((back_blocks, arrived))
        slope_mirror = mirrored(arrived[:, 1].reshape(experts * capacity, model_width), "section")
        if tick_id == 0:
            back_blocks, saved_mirror = lax.optimization_barrier((back_blocks, saved_mirror))
        returned = lax.all_to_all(back_blocks, "expert", split_axis=0, concat_axis=0, tiled=True)
        if tick_id + 1 < ticks:
            returned, slope_mirror = lax.optimization_barrier((returned, slope_mirror))
        back_rows = jnp.dot(one_hot_back, returned.reshape(-1, model_width), preferred_element_type=jnp.float32)
        finished = (current.astype(jnp.float32) + back_rows.reshape(2, tokens, model_width)).astype(
            jnp.bfloat16
        )
        if tick_id + 1 < ticks:
            from_above = passed_along(finished[0], "section", -1)
            from_below = passed_along(finished[1], "section", 1)
            current = jnp.stack([
                jnp.where(section_id == sections - 1, fresh[tick_id, 0], from_above),
                jnp.where(section_id == 0, fresh[tick_id, 1], from_below),
            ])
    hidden_m, pair_grad_m = expert_grads(
        slope_mirror, saved_mirror[ticks - 1], w_in[0, 0, 0], w_out[0, 0, 0]
    )
    part_in, part_out = weight_terms(saved_mirror[ticks - 1], slope_mirror, hidden_m, pair_grad_m)
    mirror_in = (mirror_in + part_in).astype(jnp.bfloat16).astype(jnp.float32)
    mirror_out = (mirror_out + part_out).astype(jnp.bfloat16).astype(jnp.float32)
    grad_in = (own_in + mirror_in).astype(jnp.bfloat16)
    grad_out = (own_out + mirror_out).astype(jnp.bfloat16)
    return (finished[:, None], grad_in[None, None], grad_out[None, None])


def solution(mesh):
    return jax.shard_map(
        on_device,
        mesh=mesh,
        in_specs=(
            P(None, "section", "expert", None, None),
            P(None, "section", "expert", None, None),
            P(None, "section", "expert", None),
            P(None, None, "expert", None),
            P(None, None, "section", "expert", None, None),
            P(None, None, "section", "expert"),
            P(None, None, "section", "expert"),
            P(None, None, "section", "expert", None),
        ),
        out_specs=(
            P(None, "section", "expert", None),
            P("section", "expert", None, None),
            P("section", "expert", None, None),
        ),
        check_vma=False,
    )
```

```python
import jax
import jax.numpy as jnp
from jax import lax
from jax.sharding import PartitionSpec as P


def passed_along(block, axis, distance):
    devices = range(lax.axis_size(axis))
    route = [(i - distance, i) for i in devices if i - distance in devices]
    return lax.ppermute(block, axis, route)


def mirrored(block, axis):
    count = lax.axis_size(axis)
    return lax.ppermute(block, axis, [(i, count - 1 - i) for i in range(count)])


def left_product(left, right):
    return lax.dot_general(
        left, right, (((0,), (0,)), ((), ())), preferred_element_type=jnp.float32
    )


def right_product(left, right):
    return lax.dot_general(
        left, right, (((1,), (1,)), ((), ())), preferred_element_type=jnp.float32
    )


def slot_table(route_ids, capacity, way_id, ways):
    tokens = route_ids.shape[0]
    positions = lax.iota(jnp.int32, tokens)
    earlier = (positions[None, :] < positions[:, None]) & (route_ids[None, :] == route_ids[:, None])
    within = jnp.sum(earlier.astype(jnp.int32), axis=1)
    return (route_ids * ways + way_id) * capacity + within


def placement(route_ids, capacity, experts):
    ways, tokens = route_ids.shape
    slots = jnp.concatenate(
        [slot_table(route_ids[w], capacity, w, ways) for w in range(ways)]
    )
    rows = lax.iota(jnp.int32, ways * experts * capacity)
    scatter = (rows[:, None] == slots[None, :]).astype(jnp.bfloat16)
    gather = (slots[:, None] == rows[None, :]).astype(jnp.bfloat16)
    return scatter, gather


def exchange(blocks):
    experts, ways, capacity, model_width = blocks.shape
    arrived = lax.all_to_all(blocks, "expert", split_axis=0, concat_axis=0, tiled=True)
    return [arrived[:, way_id].reshape(experts * capacity, model_width) for way_id in range(ways)]


def expert_grads(slope_rows, saved_rows, weight_in, weight_out):
    hidden_width = weight_out.shape[0]
    gate_up = jnp.dot(saved_rows, weight_in, preferred_element_type=jnp.float32)
    gate_part = gate_up[:, :hidden_width]
    upward = gate_up[:, hidden_width:]
    sigmoid_gate = jax.nn.sigmoid(gate_part)
    active = gate_part * sigmoid_gate
    hidden = (active * upward).astype(jnp.bfloat16)
    hidden_grad = right_product(slope_rows, weight_out)
    gate_grad = hidden_grad * upward * sigmoid_gate * (1.0 + gate_part * (1.0 - sigmoid_gate))
    pair_grad = jnp.concatenate([gate_grad, hidden_grad * active], axis=1).astype(jnp.bfloat16)
    return hidden, pair_grad


def weight_terms(saved_rows, slope_rows, hidden, pair_grad):
    return left_product(saved_rows, pair_grad), left_product(hidden, slope_rows)


def on_device(w_in, w_out, grads, fresh, saved, probs, routes, counts):
    sections = lax.axis_size("section")
    section_id = lax.axis_index("section")
    experts = lax.axis_size("expert")
    model_width = grads.shape[-1]
    tokens = grads.shape[2]
    capacity = 2 * tokens // experts
    hidden_width = w_out.shape[-2]
    ticks = saved.shape[0]
    saved_mirror = [mirrored(saved[tick_id, 1, 0, 0], "section") for tick_id in range(saved.shape[0])]
    current = grads[:, 0]
    zeros_in = jnp.zeros((model_width, 2 * hidden_width), jnp.float32)
    zeros_out = jnp.zeros((hidden_width, model_width), jnp.float32)
    own_in, own_out = zeros_in, zeros_out
    mirror_in, mirror_out = zeros_in, zeros_out
    slope_mirror = None
    for tick_id in range(ticks):
        one_hot, one_hot_back = placement(routes[tick_id, :, 0], capacity, experts)
        scaled = (probs[tick_id, :, 0][:, :, None] * current.astype(jnp.float32)).astype(jnp.bfloat16)
        blocks = jnp.dot(one_hot, scaled.reshape(-1, model_width), preferred_element_type=jnp.float32)
        blocks = blocks.astype(jnp.bfloat16).reshape(experts, 2, capacity, model_width)
        if slope_mirror is not None:
            hidden_m, pair_grad_m = expert_grads(
                slope_mirror, saved_mirror[tick_id - 1], w_in[0, 0, 0], w_out[0, 0, 0]
            )
            part_in, part_out = weight_terms(
                saved_mirror[tick_id - 1], slope_mirror, hidden_m, pair_grad_m
            )
            mirror_in = mirror_in + part_in
            mirror_out = mirror_out + part_out
        slopes = exchange(blocks)
        input_grads = []
        for way_id in range(2):
            saved_rows = saved[tick_id, way_id, 0, 0]
            hidden, pair_grad = expert_grads(
                slopes[way_id], saved_rows, w_in[way_id, 0, 0], w_out[way_id, 0, 0]
            )
            input_grad = right_product(pair_grad, w_in[way_id, 0, 0]).astype(jnp.bfloat16)
            input_grads.append(input_grad.reshape(experts, 1, capacity, model_width))
            if way_id == 0:
                part_in, part_out = weight_terms(saved_rows, slopes[0], hidden, pair_grad)
                own_in = own_in + part_in
                own_out = own_out + part_out
        slope_mirror = mirrored(slopes[1], "section")
        back_blocks = jnp.concatenate(input_grads, axis=1)
        if tick_id == 0:
            back_blocks, saved_mirror[0] = lax.optimization_barrier((back_blocks, saved_mirror[0]))
        returned = lax.all_to_all(back_blocks, "expert", split_axis=0, concat_axis=0, tiled=True)
        if tick_id + 1 < ticks:
            returned, slope_mirror, saved_mirror[tick_id + 1] = lax.optimization_barrier(
                (returned, slope_mirror, saved_mirror[tick_id + 1])
            )
        back_rows = jnp.dot(one_hot_back, returned.reshape(-1, model_width), preferred_element_type=jnp.float32)
        finished = (current.astype(jnp.float32) + back_rows.reshape(2, tokens, model_width)).astype(
            jnp.bfloat16
        )
        if tick_id + 1 < ticks:
            from_above = passed_along(finished[0], "section", -1)
            from_below = passed_along(finished[1], "section", 1)
            current = jnp.stack([
                jnp.where(section_id == sections - 1, fresh[tick_id, 0], from_above),
                jnp.where(section_id == 0, fresh[tick_id, 1], from_below),
            ])
    hidden_m, pair_grad_m = expert_grads(
        slope_mirror, saved_mirror[ticks - 1], w_in[0, 0, 0], w_out[0, 0, 0]
    )
    part_in, part_out = weight_terms(saved_mirror[ticks - 1], slope_mirror, hidden_m, pair_grad_m)
    mirror_in = (mirror_in + part_in).astype(jnp.bfloat16).astype(jnp.float32)
    mirror_out = (mirror_out + part_out).astype(jnp.bfloat16).astype(jnp.float32)
    grad_in = (own_in + mirror_in).astype(jnp.bfloat16)
    grad_out = (own_out + mirror_out).astype(jnp.bfloat16)
    return (finished[:, None], grad_in[None, None], grad_out[None, None])


def solution(mesh):
    return jax.shard_map(
        on_device,
        mesh=mesh,
        in_specs=(
            P(None, "section", "expert", None, None),
            P(None, "section", "expert", None, None),
            P(None, "section", "expert", None),
            P(None, None, "expert", None),
            P(None, None, "section", "expert", None, None),
            P(None, None, "section", "expert"),
            P(None, None, "section", "expert"),
            P(None, None, "section", "expert", None),
        ),
        out_specs=(
            P(None, "section", "expert", None),
            P("section", "expert", None, None),
            P("section", "expert", None, None),
        ),
        check_vma=False,
    )
```

```python
import jax
import jax.numpy as jnp
from jax import lax
from jax.sharding import PartitionSpec as P


def passed_along(block, axis, distance):
    devices = range(lax.axis_size(axis))
    route = [(i - distance, i) for i in devices if i - distance in devices]
    return lax.ppermute(block, axis, route)


def mirrored(block, axis):
    count = lax.axis_size(axis)
    return lax.ppermute(block, axis, [(i, count - 1 - i) for i in range(count)])


def left_product(left, right):
    return lax.dot_general(
        left, right, (((0,), (0,)), ((), ())), preferred_element_type=jnp.float32
    )


def right_product(left, right):
    return lax.dot_general(
        left, right, (((1,), (1,)), ((), ())), preferred_element_type=jnp.float32
    )


def slot_table(route_ids, capacity, way_id, ways):
    tokens = route_ids.shape[0]
    positions = lax.iota(jnp.int32, tokens)
    earlier = (positions[None, :] < positions[:, None]) & (route_ids[None, :] == route_ids[:, None])
    within = jnp.sum(earlier.astype(jnp.int32), axis=1)
    return (route_ids * ways + way_id) * capacity + within


def placement(route_ids, capacity, experts):
    ways, tokens = route_ids.shape
    slots = jnp.concatenate(
        [slot_table(route_ids[w], capacity, w, ways) for w in range(ways)]
    )
    rows = lax.iota(jnp.int32, ways * experts * capacity)
    scatter = (rows[:, None] == slots[None, :]).astype(jnp.bfloat16)
    gather = (slots[:, None] == rows[None, :]).astype(jnp.bfloat16)
    return scatter, gather


def exchange(blocks):
    experts, ways, capacity, model_width = blocks.shape
    arrived = lax.all_to_all(blocks, "expert", split_axis=0, concat_axis=0, tiled=True)
    return [arrived[:, way_id].reshape(experts * capacity, model_width) for way_id in range(ways)]


def expert_grads(slope_rows, saved_rows, weight_in, weight_out):
    hidden_width = weight_out.shape[0]
    gate_up = jnp.dot(saved_rows, weight_in, preferred_element_type=jnp.float32)
    gate_part = gate_up[:, :hidden_width]
    upward = gate_up[:, hidden_width:]
    sigmoid_gate = jax.nn.sigmoid(gate_part)
    active = gate_part * sigmoid_gate
    hidden = (active * upward).astype(jnp.bfloat16)
    hidden_grad = right_product(slope_rows, weight_out)
    gate_grad = hidden_grad * upward * sigmoid_gate * (1.0 + gate_part * (1.0 - sigmoid_gate))
    pair_grad = jnp.concatenate([gate_grad, hidden_grad * active], axis=1).astype(jnp.bfloat16)
    return hidden, pair_grad


def weight_terms(saved_rows, slope_rows, hidden, pair_grad):
    return left_product(saved_rows, pair_grad), left_product(hidden, slope_rows)


def on_device(w_in, w_out, grads, fresh, saved, probs, routes, counts):
    sections = lax.axis_size("section")
    section_id = lax.axis_index("section")
    experts = lax.axis_size("expert")
    model_width = grads.shape[-1]
    tokens = grads.shape[2]
    capacity = 2 * tokens // experts
    hidden_width = w_out.shape[-2]
    ticks = saved.shape[0]
    saved_mirror = mirrored(saved[:, 1, 0, 0], "section")
    current = grads[:, 0]
    zeros_in = jnp.zeros((model_width, 2 * hidden_width), jnp.float32)
    zeros_out = jnp.zeros((hidden_width, model_width), jnp.float32)
    own_in, own_out = zeros_in, zeros_out
    mirror_in, mirror_out = zeros_in, zeros_out
    slope_mirror = None
    for tick_id in range(ticks):
        one_hot, one_hot_back = placement(routes[tick_id, :, 0], capacity, experts)
        scaled = (probs[tick_id, :, 0][:, :, None] * current.astype(jnp.float32)).astype(jnp.bfloat16)
        blocks = jnp.dot(
            one_hot[:, :tokens], scaled[0], preferred_element_type=jnp.float32
        ) + jnp.dot(one_hot[:, tokens:], scaled[1], preferred_element_type=jnp.float32)
        blocks = blocks.astype(jnp.bfloat16).reshape(experts, 2, capacity, model_width)
        if slope_mirror is not None:
            hidden_m, pair_grad_m = expert_grads(
                slope_mirror, saved_mirror[tick_id - 1], w_in[0, 0, 0], w_out[0, 0, 0]
            )
            part_in, part_out = weight_terms(
                saved_mirror[tick_id - 1], slope_mirror, hidden_m, pair_grad_m
            )
            mirror_in = mirror_in + part_in
            mirror_out = mirror_out + part_out
        slopes = exchange(blocks)
        input_grads = []
        for way_id in range(2):
            saved_rows = saved[tick_id, way_id, 0, 0]
            hidden, pair_grad = expert_grads(
                slopes[way_id], saved_rows, w_in[way_id, 0, 0], w_out[way_id, 0, 0]
            )
            input_grad = right_product(pair_grad, w_in[way_id, 0, 0]).astype(jnp.bfloat16)
            input_grads.append(input_grad.reshape(experts, 1, capacity, model_width))
            if way_id == 0:
                part_in, part_out = weight_terms(saved_rows, slopes[0], hidden, pair_grad)
                own_in = own_in + part_in
                own_out = own_out + part_out
        slope_mirror = mirrored(slopes[1], "section")
        back_blocks = jnp.concatenate(input_grads, axis=1)
        if tick_id == 0:
            back_blocks, saved_mirror = lax.optimization_barrier((back_blocks, saved_mirror))
        returned = lax.all_to_all(back_blocks, "expert", split_axis=0, concat_axis=0, tiled=True)
        if tick_id + 1 < ticks:
            returned, slope_mirror = lax.optimization_barrier((returned, slope_mirror))
        back_rows = jnp.dot(one_hot_back, returned.reshape(-1, model_width), preferred_element_type=jnp.float32)
        finished = (current.astype(jnp.float32) + back_rows.reshape(2, tokens, model_width)).astype(
            jnp.bfloat16
        )
        if tick_id + 1 < ticks:
            from_above = passed_along(finished[0], "section", -1)
            from_below = passed_along(finished[1], "section", 1)
            current = jnp.stack([
                jnp.where(section_id == sections - 1, fresh[tick_id, 0], from_above),
                jnp.where(section_id == 0, fresh[tick_id, 1], from_below),
            ])
    hidden_m, pair_grad_m = expert_grads(
        slope_mirror, saved_mirror[ticks - 1], w_in[0, 0, 0], w_out[0, 0, 0]
    )
    part_in, part_out = weight_terms(saved_mirror[ticks - 1], slope_mirror, hidden_m, pair_grad_m)
    mirror_in = (mirror_in + part_in).astype(jnp.bfloat16).astype(jnp.float32)
    mirror_out = (mirror_out + part_out).astype(jnp.bfloat16).astype(jnp.float32)
    grad_in = (own_in + mirror_in).astype(jnp.bfloat16)
    grad_out = (own_out + mirror_out).astype(jnp.bfloat16)
    return (finished[:, None], grad_in[None, None], grad_out[None, None])


def solution(mesh):
    return jax.shard_map(
        on_device,
        mesh=mesh,
        in_specs=(
            P(None, "section", "expert", None, None),
            P(None, "section", "expert", None, None),
            P(None, "section", "expert", None),
            P(None, None, "expert", None),
            P(None, None, "section", "expert", None, None),
            P(None, None, "section", "expert"),
            P(None, None, "section", "expert"),
            P(None, None, "section", "expert", None),
        ),
        out_specs=(
            P(None, "section", "expert", None),
            P("section", "expert", None, None),
            P("section", "expert", None, None),
        ),
        check_vma=False,
    )
```
